32 devices in a mesh: seq: 8 (over z, y), head: 4 (over x, core).
Axes of the slice: x: 2, y: 2, z: 4, core: 2. Of those that a mesh axis runs over, the one named last changes fastest.
Arguments:
- query: bfloat16 [12288, 3072], P(('seq', 'head')), may hold values from -40 to 40
- key: bfloat16 [12288, 3072], P(('seq', 'head')), may hold values from -4 to 4
- value: bfloat16 [12288, 3072], P(('seq', 'head')), may hold values from -6 to 6
- raster_to_tile: int32 [12288], P(('seq', 'head')), may hold values from 0 to 12287, as said below
- window_list: int32 [32, 4], P('seq'), may hold values from 0 to 31, as said below
- valid_count: int32 [32], replicated, may hold values from 96 to 384
Outputs:
- attended: bfloat16 [12288, 3072], P(('seq', 'head'))
The draws below stay inside these ranges and needn't reach their ends.
Inputs may be any that keep to these rules, and one draw needn't show every extreme that they name: `raster_to_tile`: A permutation of the slots. Raster shard d (rows d * 1536 // 4 onward, d counting seq+head) holds exactly 48 slots of every owner o, where owner o holds slots o * 1536 to (o+1) * 1536 - 1. `window_list`: row t holds t first, then 4 - 1 distinct other tiles, each within 3 tiles of t.
All inputs are finite; a program needn't handle non-finite values.
Results may differ from the reference program's by a relative error of at most 0.0036.
Values may be sent and summed in bfloat16 or wider, within the bound.
No kernel may reach another device: no remote copies, remote signals or barrier semaphores. Data moves between devices by JAX's collectives and lax.ppermute only.
A program may use at most 128 MiB of HBM per device.

```python
import jax
import jax.numpy as jnp
from jax import lax

HEADS = 24
HEAD_DIM = 128
TILE = 384
WIN = 4
REACH = 3
TOK_DEV = 1536
TILES = 32
TOKENS = 12288
N_SEQ = 8
N_HEAD = 4


def tile_order(key):
    base = jax.random.fold_in(key, 7001)
    sources = N_SEQ * N_HEAD
    share = TOK_DEV // sources

    def owner_slots(owner):
        return owner * TOK_DEV + jax.random.permutation(jax.random.fold_in(base, owner), TOK_DEV)
    table = jax.vmap(owner_slots)(jnp.arange(N_SEQ, dtype=jnp.int32)).reshape(N_SEQ, sources, share)
    per_source = jnp.transpose(table, (1, 0, 2)).reshape(sources, N_SEQ * share)

    def shuffle(source, row):
        return jax.random.permutation(jax.random.fold_in(base, N_SEQ + source), row)
    mixed = jax.vmap(shuffle)(jnp.arange(sources, dtype=jnp.int32), per_source)
    return mixed.reshape(TOKENS).astype(jnp.int32)


def draw_raster_to_tile(key, part):
    return tile_order(key)


def draw_window_list(key, part):
    stream_key = jax.random.fold_in(key, 7003)
    tiles = jnp.arange(TILES, dtype=jnp.int32)
    offsets = jnp.concatenate([jnp.arange(-REACH, 0, dtype=jnp.int32), jnp.arange(1, REACH + 1, dtype=jnp.int32)])
    nearby = tiles[:, None] + offsets[None, :]
    scores = jax.random.randint(stream_key, (TILES, 2 * REACH), 0, 1000) * (2 * REACH) + jnp.arange(2 * REACH, dtype=jnp.int32)[None, :]
    scores = jnp.where((nearby >= 0) & (nearby < TILES), scores, -1)
    unused, picked = lax.top_k(scores, WIN - 1)
    chosen = jnp.take_along_axis(nearby, picked, axis=1)
    return jnp.concatenate([tiles[:, None], chosen], axis=1).astype(jnp.int32)


def draw_valid_count(key, part):
    stream_key = jax.random.fold_in(key, 7002)
    edges = jax.random.randint(jax.random.fold_in(stream_key, 1), (TILES,), 0, 4) == 0
    edges = edges & (jnp.arange(TILES, dtype=jnp.int32) > 0)
    shorter = jax.random.randint(jax.random.fold_in(stream_key, 2), (TILES,), TILE // 4, TILE)
    return jnp.where(edges, shorter, TILE).astype(jnp.int32)


def draw_query(key, part):
    stream_key = jax.random.fold_in(key, 7005)
    values = 2.0 * jax.random.truncated_normal(stream_key, -6.0, 6.0, (TOKENS, HEADS * HEAD_DIM))
    return values.astype(jnp.bfloat16)


def draw_key(key, part):
    stream_key = jax.random.fold_in(key, 7006)
    values = jax.random.truncated_normal(stream_key, -4.0, 4.0, (TOKENS, HEADS * HEAD_DIM))
    return values.astype(jnp.bfloat16)


def block_scale(key, extent, shards, smallest, largest):
    loudness = 1.0
    for axis_at, blocks in shards:
        steps = jax.random.uniform(jax.random.fold_in(jax.random.fold_in(key, 6), axis_at), (blocks,), jnp.float32, smallest / len(shards), largest / len(shards))
        loudness = loudness * jnp.repeat(jnp.exp(steps), extent[axis_at] // blocks).reshape((-1,) + (1,) * (len(extent) - 1 - axis_at))
    return loudness


def bell_draw(rng, shape, spread, bound, pieces=(), held_as=jnp.bfloat16):
    level = block_scale(rng, shape, pieces, -0.22, 0.18) if pieces else 1.0
    values = jax.random.normal(rng, shape, jnp.float32) * spread * level
    return jnp.minimum(jnp.maximum(values, -bound), bound).astype(held_as)


def setup_inputs(seed: int = 0) -> dict:
    arg_keys = jax.random.split(jax.random.key(seed), 7)
    return {
        "query": draw_query(jax.random.fold_in(arg_keys[6], 71), 0),
        "key": draw_key(jax.random.fold_in(arg_keys[6], 71), 0),
        "value": bell_draw(arg_keys[2], (TOKENS, HEADS * HEAD_DIM), 1.0, 6.0, ((0, 32),)),
        "raster_to_tile": draw_raster_to_tile(jax.random.fold_in(arg_keys[6], 71), 0),
        "window_list": draw_window_list(jax.random.fold_in(arg_keys[6], 71), 0),
        "valid_count": draw_valid_count(jax.random.fold_in(arg_keys[6], 71), 0),
    }


def reference(query, key, value, raster_to_tile, window_list, valid_count):
    slot_rows = jnp.zeros((TOKENS,), jnp.int32).at[raster_to_tile].set(jnp.arange(TOKENS, dtype=jnp.int32))
    q_tiles = query[slot_rows].reshape(TILES, TILE, HEADS, HEAD_DIM)
    k_tiles = key[slot_rows].reshape(TILES, TILE, HEADS, HEAD_DIM)
    v_tiles = value[slot_rows].reshape(TILES, TILE, HEADS, HEAD_DIM)
    slot_ok = jnp.arange(TILE, dtype=jnp.int32)[None, :] < valid_count[:, None]
    scale = HEAD_DIM ** -0.5

    def one_tile(index):
        wins = window_list[index]
        q_blk = q_tiles[index].astype(jnp.float32)
        k_blk = k_tiles[wins].reshape(WIN * TILE, HEADS, HEAD_DIM).astype(jnp.float32)
        v_blk = v_tiles[wins].reshape(WIN * TILE, HEADS, HEAD_DIM).astype(jnp.float32)
        usable = slot_ok[wins].reshape(WIN * TILE)
        scores = jnp.einsum("qhd,khd->hqk", q_blk, k_blk) * scale
        scores = jnp.where(usable[None, None, :], scores, -jnp.inf)
        top = jnp.max(scores, axis=2, keepdims=True)
        weights = jnp.exp(scores - top)
        total = jnp.sum(weights, axis=2)
        rounded = lax.optimization_barrier(weights.astype(jnp.bfloat16)).astype(jnp.float32)
        mixed = jnp.einsum("hqk,khd->qhd", rounded, v_blk)
        mixed = mixed / jnp.transpose(total)[:, :, None]
        mixed = jnp.where(slot_ok[index][:, None, None], mixed, 0.0)
        return mixed.astype(jnp.bfloat16).reshape(TILE, HEADS * HEAD_DIM)

    tiled = lax.map(one_tile, jnp.arange(TILES, dtype=jnp.int32)).reshape(TOKENS, HEADS * HEAD_DIM)
    return tiled[raster_to_tile]
```

```python
import functools

import jax
import jax.numpy as jnp
from jax import lax
from jax.experimental import pallas as pl
from jax.experimental.pallas import tpu as pltpu
from jax.sharding import PartitionSpec as P

HEAD_DIM = 128


def attn_kernel(win, tile, scale, win_ref, vcw_ref, vco_ref, q_ref, *refs):
    k_refs = refs[:win]
    v_refs = refs[win : 2 * win]
    o_ref = refs[2 * win]
    s_scr = refs[2 * win + 1]
    i = pl.program_id(0)
    q = q_ref[...]
    col = lax.broadcasted_iota(jnp.int32, (tile, tile), 1)
    for w in range(win):
        s = lax.dot_general(
            q, k_refs[w][...], (((1,), (1,)), ((), ())), preferred_element_type=jnp.float32
        )
        s = s * scale
        s = jnp.where(col < vcw_ref[i * win + w], s, -jnp.inf)
        s_scr[:, w * tile : (w + 1) * tile] = s
    s = s_scr[...]
    m = jnp.max(s, axis=1, keepdims=True)
    p = jnp.exp(s - m)
    total = jnp.sum(p, axis=1, keepdims=True)
    pb = p.astype(jnp.bfloat16)
    acc = jnp.dot(pb[:, 0:tile], v_refs[0][...], preferred_element_type=jnp.float32)
    for w in range(1, win):
        acc = acc + jnp.dot(
            pb[:, w * tile : (w + 1) * tile], v_refs[w][...], preferred_element_type=jnp.float32
        )
    out = acc / total
    row = lax.broadcasted_iota(jnp.int32, (tile, 1), 0)
    out = jnp.where(row < vco_ref[i], out, 0.0)
    o_ref[...] = out.astype(o_ref.dtype)


def attention(q_tile, kv_ext, win_flat, vcw_flat, vc_own, tile, win, heads_here):
    tok_dev, pw = q_tile.shape
    tile_dev = tok_dev // tile
    scale = HEAD_DIM ** (-0.5)

    def q_map(i, j, w_ref, a_ref, b_ref):
        return (i, j)

    def k_map(w, i, j, w_ref, a_ref, b_ref):
        return (w_ref[i * win + w], j)

    def v_map(w, i, j, w_ref, a_ref, b_ref):
        return (w_ref[i * win + w], heads_here + j)

    blk = (tile, HEAD_DIM)
    in_specs = [pl.BlockSpec(blk, q_map)]
    in_specs += [pl.BlockSpec(blk, functools.partial(k_map, w)) for w in range(win)]
    in_specs += [pl.BlockSpec(blk, functools.partial(v_map, w)) for w in range(win)]
    steps = tile_dev * heads_here
    cost = pl.CostEstimate(
        flops=steps * 4 * tile * win * tile * HEAD_DIM,
        transcendentals=steps * tile * win * tile,
        bytes_accessed=steps * (2 * win + 2) * tile * HEAD_DIM * 2,
    )
    return pl.pallas_call(
        functools.partial(attn_kernel, win, tile, scale),
        out_shape=jax.ShapeDtypeStruct((tok_dev, pw), jnp.bfloat16),
        grid_spec=pltpu.PrefetchScalarGridSpec(
            num_scalar_prefetch=3,
            grid=(tile_dev, heads_here),
            in_specs=in_specs,
            out_specs=pl.BlockSpec(blk, q_map),
            scratch_shapes=[pltpu.VMEM((tile, win * tile), jnp.float32)],
        ),
        cost_estimate=cost,
    )(win_flat, vcw_flat, vc_own, q_tile, *([kv_ext] * (2 * win)))


def body(query, key, value, raster_to_tile, window_list, valid_count):
    seq_count = lax.axis_size("seq")
    head_count = lax.axis_size("head")
    seq_pos = lax.axis_index("seq")
    rows_here, width = query.shape
    part_width = width // head_count
    tile_dev, win = window_list.shape
    tok_dev = rows_here * head_count
    tile = tok_dev // tile_dev
    share = rows_here // seq_count
    reach = win - 1
    rim = reach * tile
    ext_tiles = tile_dev + 2 * reach
    heads_here = part_width // HEAD_DIM
    all_tiles = valid_count.shape[0]

    order = jnp.argsort(raster_to_tile)
    slots_sorted = raster_to_tile[order].reshape(seq_count, share)
    joined = jnp.concatenate(
        [
            query.reshape(rows_here, head_count, part_width),
            key.reshape(rows_here, head_count, part_width),
            value.reshape(rows_here, head_count, part_width),
        ],
        axis=2,
    )
    joined_sorted = joined[order].reshape(seq_count, share, head_count, 3 * part_width)
    slot_send = jnp.broadcast_to(slots_sorted[:, :, None], (seq_count, share, head_count))

    def exchange(x):
        x = lax.all_to_all(x, "seq", split_axis=0, concat_axis=0, tiled=True)
        return lax.all_to_all(x, "head", split_axis=2, concat_axis=1, tiled=True)

    joined_in = exchange(joined_sorted).reshape(tok_dev, 3 * part_width)
    slot_in = exchange(slot_send).reshape(tok_dev)
    local = slot_in - seq_pos * tok_dev
    place = jnp.zeros((tok_dev,), jnp.int32).at[local].set(jnp.arange(tok_dev, dtype=jnp.int32))
    joined_tile = joined_in[place]
    q_tile = joined_tile[:, :part_width]
    kv_tile = joined_tile[:, part_width:]

    to_right = [(i, i + 1) for i in range(seq_count - 1)]
    to_left = [(i + 1, i) for i in range(seq_count - 1)]
    from_left = lax.ppermute(kv_tile[tok_dev - rim :], "seq", to_right)
    from_right = lax.ppermute(kv_tile[:rim], "seq", to_left)
    kv_ext = jnp.concatenate([from_left, kv_tile, from_right], axis=0)

    first_tile = seq_pos * tile_dev - reach
    global_tiles = jnp.clip(first_tile + jnp.arange(ext_tiles, dtype=jnp.int32), 0, all_tiles - 1)
    vc_ext = valid_count[global_tiles]
    local_windows = (window_list - first_tile).astype(jnp.int32)
    win_flat = local_windows.reshape(tile_dev * win)
    vcw_flat = vc_ext[local_windows].reshape(tile_dev * win)
    vc_own = vc_ext[reach : reach + tile_dev]

    out_tile = attention(q_tile, kv_ext, win_flat, vcw_flat, vc_own, tile, win, heads_here)

    outgoing = out_tile[local].reshape(seq_count, head_count, share, 1, part_width)
    arrived = lax.all_to_all(
        lax.all_to_all(outgoing, "seq", split_axis=0, concat_axis=0, tiled=True),
        "head",
        split_axis=1,
        concat_axis=3,
        tiled=True,
    )
    sorted_rows = arrived.reshape(rows_here, width)
    inverse = (
        jnp.zeros((rows_here,), jnp.int32).at[order].set(jnp.arange(rows_here, dtype=jnp.int32))
    )
    return sorted_rows[inverse]


def solution(mesh):
    placed = (
        P(("seq", "head"), None),
        P(("seq", "head"), None),
        P(("seq", "head"), None),
        P(("seq", "head")),
        P("seq", None),
        P(),
    )
    return jax.shard_map(
        body, mesh=mesh, in_specs=placed, out_specs=P(("seq", "head"), None), check_vma=False
    )
```

```python
import functools

import jax
import jax.numpy as jnp
from jax import lax
from jax.experimental import pallas as pl
from jax.experimental.pallas import tpu as pltpu
from jax.sharding import PartitionSpec as P

HEAD_DIM = 128


def attn_kernel(win, tile, scale, win_ref, vcw_ref, vco_ref, q_ref, *refs):
    k_refs = refs[:win]
    v_refs = refs[win : 2 * win]
    o_ref = refs[2 * win]
    s_scr = refs[2 * win + 1]
    i = pl.program_id(0)
    q = q_ref[...]
    col = lax.broadcasted_iota(jnp.int32, (tile, tile), 1)
    for w in range(win):
        s = lax.dot_general(
            q, k_refs[w][...], (((1,), (1,)), ((), ())), preferred_element_type=jnp.float32
        )
        s = s * scale
        s = jnp.where(col < vcw_ref[i * win + w], s, -jnp.inf)
        s_scr[:, w * tile : (w + 1) * tile] = s
    s = s_scr[...]
    m = jnp.max(s, axis=1, keepdims=True)
    p = jnp.exp(s - m)
    total = jnp.sum(p, axis=1, keepdims=True)
    pb = p.astype(jnp.bfloat16)
    acc = jnp.dot(pb[:, 0:tile], v_refs[0][...], preferred_element_type=jnp.float32)
    for w in range(1, win):
        acc = acc + jnp.dot(
            pb[:, w * tile : (w + 1) * tile], v_refs[w][...], preferred_element_type=jnp.float32
        )
    out = acc / total
    row = lax.broadcasted_iota(jnp.int32, (tile, 1), 0)
    out = jnp.where(row < vco_ref[i], out, 0.0)
    o_ref[...] = out.astype(o_ref.dtype)


def attention(q_tile, kv_ext, win_flat, vcw_flat, vc_own, tile, win, heads_here):
    tok_dev, pw = q_tile.shape
    tile_dev = tok_dev // tile
    scale = HEAD_DIM ** (-0.5)

    def q_map(i, j, w_ref, a_ref, b_ref):
        return (i, j)

    def k_map(w, i, j, w_ref, a_ref, b_ref):
        return (w_ref[i * win + w], j)

    def v_map(w, i, j, w_ref, a_ref, b_ref):
        return (w_ref[i * win + w], heads_here + j)

    blk = (tile, HEAD_DIM)
    in_specs = [pl.BlockSpec(blk, q_map)]
    in_specs += [pl.BlockSpec(blk, functools.partial(k_map, w)) for w in range(win)]
    in_specs += [pl.BlockSpec(blk, functools.partial(v_map, w)) for w in range(win)]
    steps = tile_dev * heads_here
    cost = pl.CostEstimate(
        flops=steps * 4 * tile * win * tile * HEAD_DIM,
        transcendentals=steps * tile * win * tile,
        bytes_accessed=steps * (2 * win + 2) * tile * HEAD_DIM * 2,
    )
    return pl.pallas_call(
        functools.partial(attn_kernel, win, tile, scale),
        out_shape=jax.ShapeDtypeStruct((tok_dev, pw), jnp.bfloat16),
        grid_spec=pltpu.PrefetchScalarGridSpec(
            num_scalar_prefetch=3,
            grid=(tile_dev, heads_here),
            in_specs=in_specs,
            out_specs=pl.BlockSpec(blk, q_map),
            scratch_shapes=[pltpu.VMEM((tile, win * tile), jnp.float32)],
        ),
        cost_estimate=cost,
    )(win_flat, vcw_flat, vc_own, q_tile, *([kv_ext] * (2 * win)))


def body(query, key, value, raster_to_tile, window_list, valid_count):
    seq_count = lax.axis_size("seq")
    head_count = lax.axis_size("head")
    seq_pos = lax.axis_index("seq")
    rows_here, width = query.shape
    part_width = width // head_count
    tile_dev, win = window_list.shape
    tok_dev = rows_here * head_count
    tile = tok_dev // tile_dev
    share = rows_here // seq_count
    reach = win - 1
    rim = reach * tile
    ext_tiles = tile_dev + 2 * reach
    heads_here = part_width // HEAD_DIM
    all_tiles = valid_count.shape[0]

    order = jnp.argsort(raster_to_tile)
    slots_sorted = raster_to_tile[order].reshape(seq_count, share)
    joined = jnp.concatenate(
        [
            query.reshape(rows_here, head_count, part_width),
            key.reshape(rows_here, head_count, part_width),
            value.reshape(rows_here, head_count, part_width),
        ],
        axis=2,
    )
    joined_sorted = joined[order].reshape(seq_count, share, head_count, 3 * part_width)
    slot_send = jnp.broadcast_to(slots_sorted[:, :, None], (seq_count, share, head_count))

    def exchange(x):
        lead = x.shape[1:2]
        x = jnp.swapaxes(x, 1, 2).reshape((seq_count * head_count,) + lead + x.shape[3:])
        return lax.all_to_all(x, ("seq", "head"), split_axis=0, concat_axis=0, tiled=True)

    joined_in = exchange(joined_sorted).reshape(tok_dev, 3 * part_width)
    slot_in = exchange(slot_send).reshape(tok_dev)
    local = slot_in - seq_pos * tok_dev
    place = jnp.zeros((tok_dev,), jnp.int32).at[local].set(jnp.arange(tok_dev, dtype=jnp.int32))
    joined_tile = joined_in[place]
    q_tile = joined_tile[:, :part_width]
    kv_tile = joined_tile[:, part_width:]

    to_right = [(i, i + 1) for i in range(seq_count - 1)]
    to_left = [(i + 1, i) for i in range(seq_count - 1)]
    from_left = lax.ppermute(kv_tile[tok_dev - rim :], "seq", to_right)
    from_right = lax.ppermute(kv_tile[:rim], "seq", to_left)
    kv_ext = jnp.concatenate([from_left, kv_tile, from_right], axis=0)

    first_tile = seq_pos * tile_dev - reach
    global_tiles = jnp.clip(first_tile + jnp.arange(ext_tiles, dtype=jnp.int32), 0, all_tiles - 1)
    vc_ext = valid_count[global_tiles]
    local_windows = (window_list - first_tile).astype(jnp.int32)
    win_flat = local_windows.reshape(tile_dev * win)
    vcw_flat = vc_ext[local_windows].reshape(tile_dev * win)
    vc_own = vc_ext[reach : reach + tile_dev]

    out_tile = attention(q_tile, kv_ext, win_flat, vcw_flat, vc_own, tile, win, heads_here)

    outgoing = out_tile[local].reshape(seq_count, head_count, share, 1, part_width)
    outgoing = outgoing.reshape(seq_count * head_count, share, part_width)
    arrived = lax.all_to_all(outgoing, ("seq", "head"), split_axis=0, concat_axis=0, tiled=True)
    arrived = arrived.reshape(seq_count, head_count, share, part_width)
    sorted_rows = jnp.swapaxes(arrived, 1, 2).reshape(rows_here, width)
    inverse = (
        jnp.zeros((rows_here,), jnp.int32).at[order].set(jnp.arange(rows_here, dtype=jnp.int32))
    )
    return sorted_rows[inverse]


def solution(mesh):
    placed = (
        P(("seq", "head"), None),
        P(("seq", "head"), None),
        P(("seq", "head"), None),
        P(("seq", "head")),
        P("seq", None),
        P(),
    )
    return jax.shard_map(
        body, mesh=mesh, in_specs=placed, out_specs=P(("seq", "head"), None), check_vma=False
    )
```

```python
import functools

import jax
import jax.numpy as jnp
from jax import lax
from jax.experimental import pallas as pl
from jax.experimental.pallas import tpu as pltpu
from jax.sharding import PartitionSpec as P

HEAD_DIM = 128


def attn_kernel(win, tile, scale, win_ref, vcw_ref, vco_ref, q_ref, *refs):
    k_refs = refs[:win]
    v_refs = refs[win : 2 * win]
    o_ref = refs[2 * win]
    s_scr = refs[2 * win + 1]
    i = pl.program_id(0)
    q = q_ref[...]
    col = lax.broadcasted_iota(jnp.int32, (tile, tile), 1)
    for w in range(win):
        s = lax.dot_general(
            q, k_refs[w][...], (((1,), (1,)), ((), ())), preferred_element_type=jnp.float32
        )
        s = s * scale
        s = jnp.where(col < vcw_ref[i * win + w], s, -jnp.inf)
        s_scr[:, w * tile : (w + 1) * tile] = s
    s = s_scr[...]
    m = jnp.max(s, axis=1, keepdims=True)
    p = jnp.exp(s - m)
    total = jnp.sum(p, axis=1, keepdims=True)
    pb = p.astype(jnp.bfloat16)
    acc = jnp.dot(pb[:, 0:tile], v_refs[0][...], preferred_element_type=jnp.float32)
    for w in range(1, win):
        acc = acc + jnp.dot(
            pb[:, w * tile : (w + 1) * tile], v_refs[w][...], preferred_element_type=jnp.float32
        )
    out = acc / total
    row = lax.broadcasted_iota(jnp.int32, (tile, 1), 0)
    out = jnp.where(row < vco_ref[i], out, 0.0)
    o_ref[...] = out.astype(o_ref.dtype)


def attention(q_tile, kv_ext, win_flat, vcw_flat, vc_own, tile, win, heads_here):
    tok_dev, pw = q_tile.shape
    tile_dev = tok_dev // tile
    scale = HEAD_DIM ** (-0.5)

    def q_map(i, j, w_ref, a_ref, b_ref):
        return (i, j)

    def k_map(w, i, j, w_ref, a_ref, b_ref):
        return (w_ref[i * win + w], j)

    def v_map(w, i, j, w_ref, a_ref, b_ref):
        return (w_ref[i * win + w], heads_here + j)

    blk = (tile, HEAD_DIM)
    in_specs = [pl.BlockSpec(blk, q_map)]
    in_specs += [pl.BlockSpec(blk, functools.partial(k_map, w)) for w in range(win)]
    in_specs += [pl.BlockSpec(blk, functools.partial(v_map, w)) for w in range(win)]
    steps = tile_dev * heads_here
    cost = pl.CostEstimate(
        flops=steps * 4 * tile * win * tile * HEAD_DIM,
        transcendentals=steps * tile * win * tile,
        bytes_accessed=steps * (2 * win + 2) * tile * HEAD_DIM * 2,
    )
    return pl.pallas_call(
        functools.partial(attn_kernel, win, tile, scale),
        out_shape=jax.ShapeDtypeStruct((tok_dev, pw), jnp.bfloat16),
        grid_spec=pltpu.PrefetchScalarGridSpec(
            num_scalar_prefetch=3,
            grid=(tile_dev, heads_here),
            in_specs=in_specs,
            out_specs=pl.BlockSpec(blk, q_map),
            scratch_shapes=[pltpu.VMEM((tile, win * tile), jnp.float32)],
        ),
        cost_estimate=cost,
    )(win_flat, vcw_flat, vc_own, q_tile, *([kv_ext] * (2 * win)))


def body(pos_of_owner, query, key, value, raster_to_tile, window_list, valid_count):
    seq_count = lax.axis_size("seq")
    head_count = lax.axis_size("head")
    seq_pos = lax.axis_index("seq")
    rows_here, width = query.shape
    part_width = width // head_count
    tile_dev, win = window_list.shape
    tok_dev = rows_here * head_count
    tile = tok_dev // tile_dev
    share = rows_here // seq_count
    reach = win - 1
    rim = reach * tile
    ext_tiles = tile_dev + 2 * reach
    heads_here = part_width // HEAD_DIM
    all_tiles = valid_count.shape[0]

    owner_at = [0] * seq_count
    for o, d in enumerate(pos_of_owner):
        owner_at[d] = o
    order = jnp.argsort(raster_to_tile)
    send_order = order.reshape(seq_count, share)[jnp.array(owner_at, jnp.int32)].reshape(rows_here)
    slots_sorted = raster_to_tile[send_order].reshape(seq_count, share)
    joined = jnp.concatenate(
        [
            query.reshape(rows_here, head_count, part_width),
            key.reshape(rows_here, head_count, part_width),
            value.reshape(rows_here, head_count, part_width),
        ],
        axis=2,
    )
    joined_sorted = joined[send_order].reshape(seq_count, share, head_count, 3 * part_width)
    slot_send = jnp.broadcast_to(slots_sorted[:, :, None], (seq_count, share, head_count))

    def exchange(x):
        lead = x.shape[1:2]
        x = jnp.swapaxes(x, 1, 2).reshape((seq_count * head_count,) + lead + x.shape[3:])
        return lax.all_to_all(x, ("seq", "head"), split_axis=0, concat_axis=0, tiled=True)

    joined_in = exchange(joined_sorted).reshape(tok_dev, 3 * part_width)
    slot_in = exchange(slot_send).reshape(tok_dev)
    my_owner = jnp.array(owner_at, jnp.int32)[seq_pos]
    local = slot_in - my_owner * tok_dev
    place = jnp.zeros((tok_dev,), jnp.int32).at[local].set(jnp.arange(tok_dev, dtype=jnp.int32))
    joined_tile = joined_in[place]
    q_tile = joined_tile[:, :part_width]
    kv_tile = joined_tile[:, part_width:]

    to_right = [(pos_of_owner[o], pos_of_owner[o + 1]) for o in range(seq_count - 1)]
    to_left = [(pos_of_owner[o + 1], pos_of_owner[o]) for o in range(seq_count - 1)]
    from_left = lax.ppermute(kv_tile[tok_dev - rim :], "seq", to_right)
    from_right = lax.ppermute(kv_tile[:rim], "seq", to_left)
    kv_ext = jnp.concatenate([from_left, kv_tile, from_right], axis=0)

    window_mine = lax.ppermute(
        window_list, "seq", [(o, pos_of_owner[o]) for o in range(seq_count)]
    )
    first_tile = my_owner * tile_dev - reach
    global_tiles = jnp.clip(first_tile + jnp.arange(ext_tiles, dtype=jnp.int32), 0, all_tiles - 1)
    vc_ext = valid_count[global_tiles]
    local_windows = (window_mine - first_tile).astype(jnp.int32)
    win_flat = local_windows.reshape(tile_dev * win)
    vcw_flat = vc_ext[local_windows].reshape(tile_dev * win)
    vc_own = vc_ext[reach : reach + tile_dev]

    out_tile = attention(q_tile, kv_ext, win_flat, vcw_flat, vc_own, tile, win, heads_here)

    outgoing = out_tile[local].reshape(seq_count, head_count, share, 1, part_width)
    outgoing = outgoing.reshape(seq_count * head_count, share, part_width)
    arrived = lax.all_to_all(outgoing, ("seq", "head"), split_axis=0, concat_axis=0, tiled=True)
    arrived = arrived.reshape(seq_count, head_count, share, part_width)
    sorted_rows = jnp.swapaxes(arrived, 1, 2).reshape(rows_here, width)
    inverse = (
        jnp.zeros((rows_here,), jnp.int32).at[send_order].set(jnp.arange(rows_here, dtype=jnp.int32))
    )
    return sorted_rows[inverse]


def snake(mesh):
    seq_count = mesh.shape["seq"]
    first = mesh.devices.reshape(seq_count, -1)[:, 0]
    try:
        spots = [tuple(d.coords) for d in first]
    except AttributeError:
        spots = [(0, d % 2, d // 2) for d in range(seq_count)]
    low_z = min(c[2] for c in spots)

    def rank(d):
        x, y, z = spots[d][:3]
        return (z, y if (z - low_z) % 2 == 0 else -y, x)

    return tuple(sorted(range(seq_count), key=rank))


def solution(mesh):
    placed = (
        P(("seq", "head"), None),
        P(("seq", "head"), None),
        P(("seq", "head"), None),
        P(("seq", "head")),
        P("seq", None),
        P(),
    )
    return jax.shard_map(
        functools.partial(body, snake(mesh)), mesh=mesh, in_specs=placed, out_specs=P(("seq", "head"), None), check_vma=False
    )
```

```python
import functools

import jax
import jax.numpy as jnp
from jax import lax
from jax.experimental import pallas as pl
from jax.experimental.pallas import tpu as pltpu
from jax.sharding import PartitionSpec as P

HEAD_DIM = 128


def attn_kernel(win, tile, scale, win_ref, vcw_ref, vco_ref, q_ref, *refs):
    k_refs = refs[:win]
    v_refs = refs[win : 2 * win]
    o_ref = refs[2 * win]
    s_scr = refs[2 * win + 1]
    i = pl.program_id(0)
    q = q_ref[...]
    col = lax.broadcasted_iota(jnp.int32, (tile, tile), 1)
    for w in range(win):
        s = lax.dot_general(
            q, k_refs[w][...], (((1,), (1,)), ((), ())), preferred_element_type=jnp.float32
        )
        s = s * scale
        s = jnp.where(col < vcw_ref[i * win + w], s, -jnp.inf)
        s_scr[:, w * tile : (w + 1) * tile] = s
    s = s_scr[...]
    m = jnp.max(s, axis=1, keepdims=True)
    p = jnp.exp(s - m)
    total = jnp.sum(p, axis=1, keepdims=True)
    pb = p.astype(jnp.bfloat16)
    acc = jnp.dot(pb[:, 0:tile], v_refs[0][...], preferred_element_type=jnp.float32)
    for w in range(1, win):
        acc = acc + jnp.dot(
            pb[:, w * tile : (w + 1) * tile], v_refs[w][...], preferred_element_type=jnp.float32
        )
    out = acc / total
    row = lax.broadcasted_iota(jnp.int32, (tile, 1), 0)
    out = jnp.where(row < vco_ref[i], out, 0.0)
    o_ref[...] = out.astype(o_ref.dtype)


def attention(q_tile, kv_ext, win_flat, vcw_flat, vc_own, tile, win, heads_here):
    tok_dev, pw = q_tile.shape
    tile_dev = tok_dev // tile
    scale = HEAD_DIM ** (-0.5)

    def q_map(i, j, w_ref, a_ref, b_ref):
        return (i, j)

    def k_map(w, i, j, w_ref, a_ref, b_ref):
        return (w_ref[i * win + w], j)

    def v_map(w, i, j, w_ref, a_ref, b_ref):
        return (w_ref[i * win + w], heads_here + j)

    blk = (tile, HEAD_DIM)
    in_specs = [pl.BlockSpec(blk, q_map)]
    in_specs += [pl.BlockSpec(blk, functools.partial(k_map, w)) for w in range(win)]
    in_specs += [pl.BlockSpec(blk, functools.partial(v_map, w)) for w in range(win)]
    steps = tile_dev * heads_here
    cost = pl.CostEstimate(
        flops=steps * 4 * tile * win * tile * HEAD_DIM,
        transcendentals=steps * tile * win * tile,
        bytes_accessed=steps * (2 * win + 2) * tile * HEAD_DIM * 2,
    )
    return pl.pallas_call(
        functools.partial(attn_kernel, win, tile, scale),
        out_shape=jax.ShapeDtypeStruct((tok_dev, pw), jnp.bfloat16),
        grid_spec=pltpu.PrefetchScalarGridSpec(
            num_scalar_prefetch=3,
            grid=(tile_dev, heads_here),
            in_specs=in_specs,
            out_specs=pl.BlockSpec(blk, q_map),
            scratch_shapes=[pltpu.VMEM((tile, win * tile), jnp.float32)],
        ),
        cost_estimate=cost,
    )(win_flat, vcw_flat, vc_own, q_tile, *([kv_ext] * (2 * win)))


def body(pos_of_owner, query, key, value, raster_to_tile, window_list, valid_count):
    seq_count = lax.axis_size("seq")
    head_count = lax.axis_size("head")
    seq_pos = lax.axis_index("seq")
    rows_here, width = query.shape
    part_width = width // head_count
    tile_dev, win = window_list.shape
    tok_dev = rows_here * head_count
    tile = tok_dev // tile_dev
    share = rows_here // seq_count
    reach = win - 1
    rim = reach * tile
    ext_tiles = tile_dev + 2 * reach
    heads_here = part_width // HEAD_DIM
    all_tiles = valid_count.shape[0]
    chunks = 2 if heads_here % 2 == 0 else 1
    chunk_heads = heads_here // chunks
    chunk_width = chunk_heads * HEAD_DIM
    devices = seq_count * head_count

    owner_at = [0] * seq_count
    for o, d in enumerate(pos_of_owner):
        owner_at[d] = o
    order = jnp.argsort(raster_to_tile)
    send_order = order.reshape(seq_count, share)[jnp.array(owner_at, jnp.int32)].reshape(rows_here)
    slots_sorted = raster_to_tile[send_order].reshape(seq_count, share)
    slot_send = jnp.broadcast_to(slots_sorted[:, None, :], (seq_count, head_count, share))
    slot_in = lax.all_to_all(
        slot_send.reshape(devices, share), ("seq", "head"), split_axis=0, concat_axis=0, tiled=True
    ).reshape(tok_dev)
    my_owner = jnp.array(owner_at, jnp.int32)[seq_pos]
    local = slot_in - my_owner * tok_dev
    place = jnp.zeros((tok_dev,), jnp.int32).at[local].set(jnp.arange(tok_dev, dtype=jnp.int32))

    window_mine = lax.ppermute(
        window_list, "seq", [(o, pos_of_owner[o]) for o in range(seq_count)]
    )
    first_tile = my_owner * tile_dev - reach
    global_tiles = jnp.clip(first_tile + jnp.arange(ext_tiles, dtype=jnp.int32), 0, all_tiles - 1)
    vc_ext = valid_count[global_tiles]
    local_windows = (window_mine - first_tile).astype(jnp.int32)
    win_flat = local_windows.reshape(tile_dev * win)
    vcw_flat = vc_ext[local_windows].reshape(tile_dev * win)
    vc_own = vc_ext[reach : reach + tile_dev]

    to_right = [(pos_of_owner[o], pos_of_owner[o + 1]) for o in range(seq_count - 1)]
    to_left = [(pos_of_owner[o + 1], pos_of_owner[o]) for o in range(seq_count - 1)]

    rows_sorted = [x[send_order].reshape(seq_count, share, head_count, chunks, chunk_width) for x in (query, key, value)]
    arrived = []
    for c in range(chunks):
        send = jnp.concatenate([x[:, :, :, c, :] for x in rows_sorted], axis=3)
        send = jnp.swapaxes(send, 1, 2).reshape(devices, share, 3 * chunk_width)
        got = lax.all_to_all(send, ("seq", "head"), split_axis=0, concat_axis=0, tiled=True)
        got_tile = got.reshape(tok_dev, 3 * chunk_width)[place]
        q_tile = got_tile[:, :chunk_width]
        kv_tile = got_tile[:, chunk_width:]
        from_left = lax.ppermute(kv_tile[tok_dev - rim :], "seq", to_right)
        from_right = lax.ppermute(kv_tile[:rim], "seq", to_left)
        kv_ext = jnp.concatenate([from_left, kv_tile, from_right], axis=0)
        out_tile = attention(q_tile, kv_ext, win_flat, vcw_flat, vc_own, tile, win, chunk_heads)
        outgoing = out_tile[local].reshape(devices, share, chunk_width)
        back = lax.all_to_all(outgoing, ("seq", "head"), split_axis=0, concat_axis=0, tiled=True)
        arrived.append(back.reshape(seq_count, head_count, share, 1, chunk_width))
    arrived = jnp.concatenate(arrived, axis=3)
    sorted_rows = jnp.swapaxes(arrived, 1, 2).reshape(rows_here, width)
    inverse = (
        jnp.zeros((rows_here,), jnp.int32).at[send_order].set(jnp.arange(rows_here, dtype=jnp.int32))
    )
    return sorted_rows[inverse]


def snake(mesh):
    seq_count = mesh.shape["seq"]
    first = mesh.devices.reshape(seq_count, -1)[:, 0]
    try:
        spots = [tuple(d.coords) for d in first]
    except AttributeError:
        spots = [(0, d % 2, d // 2) for d in range(seq_count)]
    low_z = min(c[2] for c in spots)

    def rank(d):
        x, y, z = spots[d][:3]
        return (z, y if (z - low_z) % 2 == 0 else -y, x)

    return tuple(sorted(range(seq_count), key=rank))


def solution(mesh):
    placed = (
        P(("seq", "head"), None),
        P(("seq", "head"), None),
        P(("seq", "head"), None),
        P(("seq", "head")),
        P("seq", None),
        P(),
    )
    return jax.shard_map(
        functools.partial(body, snake(mesh)), mesh=mesh, in_specs=placed, out_specs=P(("seq", "head"), None), check_vma=False
    )
```

```python
import functools

import jax
import jax.numpy as jnp
from jax import lax
from jax.experimental import pallas as pl
from jax.experimental.pallas import tpu as pltpu
from jax.sharding import PartitionSpec as P

HEAD_DIM = 128


def attn_kernel(win, tile, scale, win_ref, vcw_ref, vco_ref, q_ref, *refs):
    k_refs = refs[:win]
    v_refs = refs[win : 2 * win]
    o_ref = refs[2 * win]
    s_scr = refs[2 * win + 1]
    i = pl.program_id(0)
    q = q_ref[...]
    col = lax.broadcasted_iota(jnp.int32, (tile, tile), 1)
    for w in range(win):
        s = lax.dot_general(
            q, k_refs[w][...], (((1,), (1,)), ((), ())), preferred_element_type=jnp.float32
        )
        s = s * scale
        s = jnp.where(col < vcw_ref[i * win + w], s, -jnp.inf)
        s_scr[:, w * tile : (w + 1) * tile] = s
    s = s_scr[...]
    m = jnp.max(s, axis=1, keepdims=True)
    p = jnp.exp(s - m)
    total = jnp.sum(p, axis=1, keepdims=True)
    pb = p.astype(jnp.bfloat16)
    acc = jnp.dot(pb[:, 0:tile], v_refs[0][...], preferred_element_type=jnp.float32)
    for w in range(1, win):
        acc = acc + jnp.dot(
            pb[:, w * tile : (w + 1) * tile], v_refs[w][...], preferred_element_type=jnp.float32
        )
    out = acc / total
    row = lax.broadcasted_iota(jnp.int32, (tile, 1), 0)
    out = jnp.where(row < vco_ref[i], out, 0.0)
    o_ref[...] = out.astype(o_ref.dtype)


def attention(q_tile, kv_ext, win_flat, vcw_flat, vc_own, tile, win, heads_here):
    tok_dev, pw = q_tile.shape
    tile_dev = tok_dev // tile
    scale = HEAD_DIM ** (-0.5)

    def q_map(i, j, w_ref, a_ref, b_ref):
        return (i, j)

    def k_map(w, i, j, w_ref, a_ref, b_ref):
        return (w_ref[i * win + w], j)

    def v_map(w, i, j, w_ref, a_ref, b_ref):
        return (w_ref[i * win + w], heads_here + j)

    blk = (tile, HEAD_DIM)
    in_specs = [pl.BlockSpec(blk, q_map)]
    in_specs += [pl.BlockSpec(blk, functools.partial(k_map, w)) for w in range(win)]
    in_specs += [pl.BlockSpec(blk, functools.partial(v_map, w)) for w in range(win)]
    steps = tile_dev * heads_here
    cost = pl.CostEstimate(
        flops=steps * 4 * tile * win * tile * HEAD_DIM,
        transcendentals=steps * tile * win * tile,
        bytes_accessed=steps * (2 * win + 2) * tile * HEAD_DIM * 2,
    )
    return pl.pallas_call(
        functools.partial(attn_kernel, win, tile, scale),
        out_shape=jax.ShapeDtypeStruct((tok_dev, pw), jnp.bfloat16),
        grid_spec=pltpu.PrefetchScalarGridSpec(
            num_scalar_prefetch=3,
            grid=(tile_dev, heads_here),
            in_specs=in_specs,
            out_specs=pl.BlockSpec(blk, q_map),
            scratch_shapes=[pltpu.VMEM((tile, win * tile), jnp.float32)],
        ),
        cost_estimate=cost,
    )(win_flat, vcw_flat, vc_own, q_tile, *([kv_ext] * (2 * win)))


def pack_kernel(head_count, part_width, chunk_width, c, q_ref, k_ref, v_ref, o_ref):
    for h in range(head_count):
        base = h * part_width + c * chunk_width
        for t, x_ref in enumerate((q_ref, k_ref, v_ref)):
            o_ref[h, :, t * chunk_width : (t + 1) * chunk_width] = x_ref[:, base : base + chunk_width]


def pack(xs, c, seq_count, head_count, share, chunk_width):
    rows_here, width = xs[0].shape
    part_width = width // head_count
    return pl.pallas_call(
        functools.partial(pack_kernel, head_count, part_width, chunk_width, c),
        out_shape=jax.ShapeDtypeStruct((seq_count * head_count, share, 3 * chunk_width), xs[0].dtype),
        grid=(seq_count,),
        in_specs=[pl.BlockSpec((share, width), lambda s: (s, 0))] * 3,
        out_specs=pl.BlockSpec((head_count, share, 3 * chunk_width), lambda s: (s, 0, 0)),
        cost_estimate=pl.CostEstimate(
            flops=0, transcendentals=0, bytes_accessed=2 * 3 * rows_here * head_count * chunk_width * 2
        ),
    )(*xs)


def body(pos_of_owner, query, key, value, raster_to_tile, window_list, valid_count):
    seq_count = lax.axis_size("seq")
    head_count = lax.axis_size("head")
    seq_pos = lax.axis_index("seq")
    rows_here, width = query.shape
    part_width = width // head_count
    tile_dev, win = window_list.shape
    tok_dev = rows_here * head_count
    tile = tok_dev // tile_dev
    share = rows_here // seq_count
    reach = win - 1
    rim = reach * tile
    ext_tiles = tile_dev + 2 * reach
    heads_here = part_width // HEAD_DIM
    all_tiles = valid_count.shape[0]
    chunks = 2 if heads_here % 2 == 0 else 1
    chunk_heads = heads_here // chunks
    chunk_width = chunk_heads * HEAD_DIM
    devices = seq_count * head_count

    owner_at = [0] * seq_count
    for o, d in enumerate(pos_of_owner):
        owner_at[d] = o
    order = jnp.argsort(raster_to_tile)
    send_order = order.reshape(seq_count, share)[jnp.array(owner_at, jnp.int32)].reshape(rows_here)
    slots_sorted = raster_to_tile[send_order].reshape(seq_count, share)
    slot_send = jnp.broadcast_to(slots_sorted[:, None, :], (seq_count, head_count, share))
    slot_in = lax.all_to_all(
        slot_send.reshape(devices, share), ("seq", "head"), split_axis=0, concat_axis=0, tiled=True
    ).reshape(tok_dev)
    my_owner = jnp.array(owner_at, jnp.int32)[seq_pos]
    local = slot_in - my_owner * tok_dev
    place = jnp.zeros((tok_dev,), jnp.int32).at[local].set(jnp.arange(tok_dev, dtype=jnp.int32))

    window_mine = lax.ppermute(
        window_list, "seq", [(o, pos_of_owner[o]) for o in range(seq_count)]
    )
    first_tile = my_owner * tile_dev - reach
    global_tiles = jnp.clip(first_tile + jnp.arange(ext_tiles, dtype=jnp.int32), 0, all_tiles - 1)
    vc_ext = valid_count[global_tiles]
    local_windows = (window_mine - first_tile).astype(jnp.int32)
    win_flat = local_windows.reshape(tile_dev * win)
    vcw_flat = vc_ext[local_windows].reshape(tile_dev * win)
    vc_own = vc_ext[reach : reach + tile_dev]

    to_right = [(pos_of_owner[o], pos_of_owner[o + 1]) for o in range(seq_count - 1)]
    to_left = [(pos_of_owner[o + 1], pos_of_owner[o]) for o in range(seq_count - 1)]

    packable = share % 16 == 0
    if packable:
        rows_flat = [x[send_order] for x in (query, key, value)]
    else:
        rows_sorted = [
            x[send_order].reshape(seq_count, share, head_count, chunks, chunk_width)
            for x in (query, key, value)
        ]
    arrived = []
    for c in range(chunks):
        if packable:
            send = pack(rows_flat, c, seq_count, head_count, share, chunk_width)
        else:
            send = jnp.concatenate([x[:, :, :, c, :] for x in rows_sorted], axis=3)
            send = jnp.swapaxes(send, 1, 2).reshape(devices, share, 3 * chunk_width)
        got = lax.all_to_all(send, ("seq", "head"), split_axis=0, concat_axis=0, tiled=True)
        got_tile = got.reshape(tok_dev, 3 * chunk_width)[place]
        q_tile = got_tile[:, :chunk_width]
        kv_tile = got_tile[:, chunk_width:]
        from_left = lax.ppermute(kv_tile[tok_dev - rim :], "seq", to_right)
        from_right = lax.ppermute(kv_tile[:rim], "seq", to_left)
        kv_ext = jnp.concatenate([from_left, kv_tile, from_right], axis=0)
        out_tile = attention(q_tile, kv_ext, win_flat, vcw_flat, vc_own, tile, win, chunk_heads)
        outgoing = out_tile[local].reshape(devices, share, chunk_width)
        back = lax.all_to_all(outgoing, ("seq", "head"), split_axis=0, concat_axis=0, tiled=True)
        arrived.append(back.reshape(seq_count, head_count, share, 1, chunk_width))
    arrived = jnp.concatenate(arrived, axis=3)
    sorted_rows = jnp.swapaxes(arrived, 1, 2).reshape(rows_here, width)
    inverse = (
        jnp.zeros((rows_here,), jnp.int32).at[send_order].set(jnp.arange(rows_here, dtype=jnp.int32))
    )
    return sorted_rows[inverse]


def snake(mesh):
    seq_count = mesh.shape["seq"]
    first = mesh.devices.reshape(seq_count, -1)[:, 0]
    try:
        spots = [tuple(d.coords) for d in first]
    except AttributeError:
        spots = [(0, d % 2, d // 2) for d in range(seq_count)]
    low_z = min(c[2] for c in spots)

    def rank(d):
        x, y, z = spots[d][:3]
        return (z, y if (z - low_z) % 2 == 0 else -y, x)

    return tuple(sorted(range(seq_count), key=rank))


def solution(mesh):
    placed = (
        P(("seq", "head"), None),
        P(("seq", "head"), None),
        P(("seq", "head"), None),
        P(("seq", "head")),
        P("seq", None),
        P(),
    )
    return jax.shard_map(
        functools.partial(body, snake(mesh)), mesh=mesh, in_specs=placed, out_specs=P(("seq", "head"), None), check_vma=False
    )
```

```python
import functools

import jax
import jax.numpy as jnp
from jax import lax
from jax.experimental import pallas as pl
from jax.experimental.pallas import tpu as pltpu
from jax.sharding import PartitionSpec as P

HEAD_DIM = 128


def attn_kernel(win, tile, scale, win_ref, vcw_ref, vco_ref, q_ref, *refs):
    k_refs = refs[:win]
    v_refs = refs[win : 2 * win]
    o_ref = refs[2 * win]
    s_scr = refs[2 * win + 1]
    i = pl.program_id(0)
    q = q_ref[...]
    col = lax.broadcasted_iota(jnp.int32, (tile, tile), 1)
    for w in range(win):
        s = lax.dot_general(
            q, k_refs[w][...], (((1,), (1,)), ((), ())), preferred_element_type=jnp.float32
        )
        s = s * scale
        s = jnp.where(col < vcw_ref[i * win + w], s, -jnp.inf)
        s_scr[:, w * tile : (w + 1) * tile] = s
    s = s_scr[...]
    m = jnp.max(s, axis=1, keepdims=True)
    p = jnp.exp(s - m)
    total = jnp.sum(p, axis=1, keepdims=True)
    pb = p.astype(jnp.bfloat16)
    acc = jnp.dot(pb[:, 0:tile], v_refs[0][...], preferred_element_type=jnp.float32)
    for w in range(1, win):
        acc = acc + jnp.dot(
            pb[:, w * tile : (w + 1) * tile], v_refs[w][...], preferred_element_type=jnp.float32
        )
    out = acc / total
    row = lax.broadcasted_iota(jnp.int32, (tile, 1), 0)
    out = jnp.where(row < vco_ref[i], out, 0.0)
    o_ref[...] = out.astype(o_ref.dtype)


def attention(q_tile, kv_ext, win_flat, vcw_flat, vc_own, tile, win, heads_here):
    tok_dev, pw = q_tile.shape
    tile_dev = tok_dev // tile
    scale = HEAD_DIM ** (-0.5)

    def q_map(i, j, w_ref, a_ref, b_ref):
        return (i, j)

    def k_map(w, i, j, w_ref, a_ref, b_ref):
        return (w_ref[i * win + w], j)

    def v_map(w, i, j, w_ref, a_ref, b_ref):
        return (w_ref[i * win + w], heads_here + j)

    blk = (tile, HEAD_DIM)
    in_specs = [pl.BlockSpec(blk, q_map)]
    in_specs += [pl.BlockSpec(blk, functools.partial(k_map, w)) for w in range(win)]
    in_specs += [pl.BlockSpec(blk, functools.partial(v_map, w)) for w in range(win)]
    steps = tile_dev * heads_here
    cost = pl.CostEstimate(
        flops=steps * 4 * tile * win * tile * HEAD_DIM,
        transcendentals=steps * tile * win * tile,
        bytes_accessed=steps * (2 * win + 2) * tile * HEAD_DIM * 2,
    )
    return pl.pallas_call(
        functools.partial(attn_kernel, win, tile, scale),
        out_shape=jax.ShapeDtypeStruct((tok_dev, pw), jnp.bfloat16),
        grid_spec=pltpu.PrefetchScalarGridSpec(
            num_scalar_prefetch=3,
            grid=(tile_dev, heads_here),
            in_specs=in_specs,
            out_specs=pl.BlockSpec(blk, q_map),
            scratch_shapes=[pltpu.VMEM((tile, win * tile), jnp.float32)],
        ),
        cost_estimate=cost,
    )(win_flat, vcw_flat, vc_own, q_tile, *([kv_ext] * (2 * win)))


def pack_kernel(head_count, part_width, chunk_width, c, q_ref, k_ref, v_ref, o_ref):
    for h in range(head_count):
        base = h * part_width + c * chunk_width
        for t, x_ref in enumerate((q_ref, k_ref, v_ref)):
            o_ref[h, :, t * chunk_width : (t + 1) * chunk_width] = x_ref[:, base : base + chunk_width]


def pack(xs, c, seq_count, head_count, share, chunk_width):
    rows_here, width = xs[0].shape
    part_width = width // head_count
    return pl.pallas_call(
        functools.partial(pack_kernel, head_count, part_width, chunk_width, c),
        out_shape=jax.ShapeDtypeStruct((seq_count * head_count, share, 3 * chunk_width), xs[0].dtype),
        grid=(seq_count,),
        in_specs=[pl.BlockSpec((share, width), lambda s: (s, 0))] * 3,
        out_specs=pl.BlockSpec((head_count, share, 3 * chunk_width), lambda s: (s, 0, 0)),
        cost_estimate=pl.CostEstimate(
            flops=0, transcendentals=0, bytes_accessed=2 * 3 * rows_here * head_count * chunk_width * 2
        ),
    )(*xs)


def unpack_kernel(head_count, part_width, chunk_width, *refs):
    o_ref = refs[-1]
    for c, b_ref in enumerate(refs[:-1]):
        for h in range(head_count):
            base = h * part_width + c * chunk_width
            o_ref[:, base : base + chunk_width] = b_ref[h]


def unpack(backs, seq_count, head_count, share, width):
    devices, _, chunk_width = backs[0].shape
    part_width = width // head_count
    return pl.pallas_call(
        functools.partial(unpack_kernel, head_count, part_width, chunk_width),
        out_shape=jax.ShapeDtypeStruct((seq_count * share, width), backs[0].dtype),
        grid=(seq_count,),
        in_specs=[pl.BlockSpec((head_count, share, chunk_width), lambda s: (s, 0, 0))] * len(backs),
        out_specs=pl.BlockSpec((share, width), lambda s: (s, 0)),
        cost_estimate=pl.CostEstimate(
            flops=0, transcendentals=0, bytes_accessed=2 * seq_count * share * width * 2
        ),
    )(*backs)


def body(pos_of_owner, query, key, value, raster_to_tile, window_list, valid_count):
    seq_count = lax.axis_size("seq")
    head_count = lax.axis_size("head")
    seq_pos = lax.axis_index("seq")
    rows_here, width = query.shape
    part_width = width // head_count
    tile_dev, win = window_list.shape
    tok_dev = rows_here * head_count
    tile = tok_dev // tile_dev
    share = rows_here // seq_count
    reach = win - 1
    rim = reach * tile
    ext_tiles = tile_dev + 2 * reach
    heads_here = part_width // HEAD_DIM
    all_tiles = valid_count.shape[0]
    chunks = 3 if heads_here % 3 == 0 else (2 if heads_here % 2 == 0 else 1)
    chunk_heads = heads_here // chunks
    chunk_width = chunk_heads * HEAD_DIM
    devices = seq_count * head_count

    owner_at = [0] * seq_count
    for o, d in enumerate(pos_of_owner):
        owner_at[d] = o
    order = jnp.argsort(raster_to_tile)
    send_order = order.reshape(seq_count, share)[jnp.array(owner_at, jnp.int32)].reshape(rows_here)
    slots_sorted = raster_to_tile[send_order].reshape(seq_count, share)
    slot_send = jnp.broadcast_to(slots_sorted[:, None, :], (seq_count, head_count, share))
    slot_in = lax.all_to_all(
        slot_send.reshape(devices, share), ("seq", "head"), split_axis=0, concat_axis=0, tiled=True
    ).reshape(tok_dev)
    my_owner = jnp.array(owner_at, jnp.int32)[seq_pos]
    local = slot_in - my_owner * tok_dev
    place = jnp.zeros((tok_dev,), jnp.int32).at[local].set(jnp.arange(tok_dev, dtype=jnp.int32))

    window_mine = lax.ppermute(
        window_list, "seq", [(o, pos_of_owner[o]) for o in range(seq_count)]
    )
    first_tile = my_owner * tile_dev - reach
    global_tiles = jnp.clip(first_tile + jnp.arange(ext_tiles, dtype=jnp.int32), 0, all_tiles - 1)
    vc_ext = valid_count[global_tiles]
    local_windows = (window_mine - first_tile).astype(jnp.int32)
    win_flat = local_windows.reshape(tile_dev * win)
    vcw_flat = vc_ext[local_windows].reshape(tile_dev * win)
    vc_own = vc_ext[reach : reach + tile_dev]

    to_right = [(pos_of_owner[o], pos_of_owner[o + 1]) for o in range(seq_count - 1)]
    to_left = [(pos_of_owner[o + 1], pos_of_owner[o]) for o in range(seq_count - 1)]

    packable = share % 16 == 0
    if packable:
        rows_flat = [x[send_order] for x in (query, key, value)]
    else:
        rows_sorted = [
            x[send_order].reshape(seq_count, share, head_count, chunks, chunk_width)
            for x in (query, key, value)
        ]
    arrived = []
    for c in range(chunks):
        if packable:
            send = pack(rows_flat, c, seq_count, head_count, share, chunk_width)
        else:
            send = jnp.concatenate([x[:, :, :, c, :] for x in rows_sorted], axis=3)
            send = jnp.swapaxes(send, 1, 2).reshape(devices, share, 3 * chunk_width)
        got = lax.all_to_all(send, ("seq", "head"), split_axis=0, concat_axis=0, tiled=True)
        got_tile = got.reshape(tok_dev, 3 * chunk_width)[place]
        q_tile = got_tile[:, :chunk_width]
        kv_tile = got_tile[:, chunk_width:]
        from_left = lax.ppermute(kv_tile[tok_dev - rim :], "seq", to_right)
        from_right = lax.ppermute(kv_tile[:rim], "seq", to_left)
        kv_ext = jnp.concatenate([from_left, kv_tile, from_right], axis=0)
        out_tile = attention(q_tile, kv_ext, win_flat, vcw_flat, vc_own, tile, win, chunk_heads)
        outgoing = out_tile[local].reshape(devices, share, chunk_width)
        back = lax.all_to_all(outgoing, ("seq", "head"), split_axis=0, concat_axis=0, tiled=True)
        arrived.append(back)
    if packable:
        sorted_rows = unpack(arrived, seq_count, head_count, share, width)
    else:
        arrived = [b.reshape(seq_count, head_count, share, 1, chunk_width) for b in arrived]
        arrived = jnp.concatenate(arrived, axis=3)
        sorted_rows = jnp.swapaxes(arrived, 1, 2).reshape(rows_here, width)
    inverse = (
        jnp.zeros((rows_here,), jnp.int32).at[send_order].set(jnp.arange(rows_here, dtype=jnp.int32))
    )
    return sorted_rows[inverse]


def snake(mesh):
    seq_count = mesh.shape["seq"]
    first = mesh.devices.reshape(seq_count, -1)[:, 0]
    try:
        spots = [tuple(d.coords) for d in first]
    except AttributeError:
        spots = [(0, d % 2, d // 2) for d in range(seq_count)]
    low_z = min(c[2] for c in spots)

    def rank(d):
        x, y, z = spots[d][:3]
        return (z, y if (z - low_z) % 2 == 0 else -y, x)

    return tuple(sorted(range(seq_count), key=rank))


def solution(mesh):
    placed = (
        P(("seq", "head"), None),
        P(("seq", "head"), None),
        P(("seq", "head"), None),
        P(("seq", "head")),
        P("seq", None),
        P(),
    )
    return jax.shard_map(
        functools.partial(body, snake(mesh)), mesh=mesh, in_specs=placed, out_specs=P(("seq", "head"), None), check_vma=False
    )
```

```python
import functools

import jax
import jax.numpy as jnp
from jax import lax
from jax.experimental import pallas as pl
from jax.experimental.pallas import tpu as pltpu
from jax.sharding import PartitionSpec as P

HEAD_DIM = 128


def attn_kernel(win, tile, scale, win_ref, vcw_ref, vco_ref, q_ref, *refs):
    k_refs = refs[:win]
    v_refs = refs[win : 2 * win]
    o_ref = refs[2 * win]
    s_scr = refs[2 * win + 1]
    i = pl.program_id(0)
    q = q_ref[...]
    col = lax.broadcasted_iota(jnp.int32, (tile, tile), 1)
    for w in range(win):
        s = lax.dot_general(
            q, k_refs[w][...], (((1,), (1,)), ((), ())), preferred_element_type=jnp.float32
        )
        s = s * scale
        s = jnp.where(col < vcw_ref[i * win + w], s, -jnp.inf)
        s_scr[:, w * tile : (w + 1) * tile] = s
    s = s_scr[...]
    m = jnp.max(s, axis=1, keepdims=True)
    p = jnp.exp(s - m)
    total = jnp.sum(p, axis=1, keepdims=True)
    pb = p.astype(jnp.bfloat16)
    acc = jnp.dot(pb[:, 0:tile], v_refs[0][...], preferred_element_type=jnp.float32)
    for w in range(1, win):
        acc = acc + jnp.dot(
            pb[:, w * tile : (w + 1) * tile], v_refs[w][...], preferred_element_type=jnp.float32
        )
    out = acc / total
    row = lax.broadcasted_iota(jnp.int32, (tile, 1), 0)
    out = jnp.where(row < vco_ref[i], out, 0.0)
    o_ref[...] = out.astype(o_ref.dtype)


def attention(q_tile, kv_ext, win_flat, vcw_flat, vc_own, tile, win, heads_here):
    tok_dev, pw = q_tile.shape
    tile_dev = tok_dev // tile
    scale = HEAD_DIM ** (-0.5)

    def q_map(i, j, w_ref, a_ref, b_ref):
        return (i, j)

    def k_map(w, i, j, w_ref, a_ref, b_ref):
        return (w_ref[i * win + w], j)

    def v_map(w, i, j, w_ref, a_ref, b_ref):
        return (w_ref[i * win + w], heads_here + j)

    blk = (tile, HEAD_DIM)
    in_specs = [pl.BlockSpec(blk, q_map)]
    in_specs += [pl.BlockSpec(blk, functools.partial(k_map, w)) for w in range(win)]
    in_specs += [pl.BlockSpec(blk, functools.partial(v_map, w)) for w in range(win)]
    steps = tile_dev * heads_here
    cost = pl.CostEstimate(
        flops=steps * 4 * tile * win * tile * HEAD_DIM,
        transcendentals=steps * tile * win * tile,
        bytes_accessed=steps * (2 * win + 2) * tile * HEAD_DIM * 2,
    )
    return pl.pallas_call(
        functools.partial(attn_kernel, win, tile, scale),
        out_shape=jax.ShapeDtypeStruct((tok_dev, pw), jnp.bfloat16),
        grid_spec=pltpu.PrefetchScalarGridSpec(
            num_scalar_prefetch=3,
            grid=(tile_dev, heads_here),
            in_specs=in_specs,
            out_specs=pl.BlockSpec(blk, q_map),
            scratch_shapes=[pltpu.VMEM((tile, win * tile), jnp.float32)],
        ),
        cost_estimate=cost,
    )(win_flat, vcw_flat, vc_own, q_tile, *([kv_ext] * (2 * win)))


def pack_kernel(head_count, part_width, chunk_width, c, q_ref, k_ref, v_ref, o_ref):
    for h in range(head_count):
        base = h * part_width + c * chunk_width
        for t, x_ref in enumerate((q_ref, k_ref, v_ref)):
            o_ref[h, :, t * chunk_width : (t + 1) * chunk_width] = x_ref[:, base : base + chunk_width]


def pack(xs, c, seq_count, head_count, share, chunk_width):
    rows_here, width = xs[0].shape
    part_width = width // head_count
    return pl.pallas_call(
        functools.partial(pack_kernel, head_count, part_width, chunk_width, c),
        out_shape=jax.ShapeDtypeStruct((seq_count * head_count, share, 3 * chunk_width), xs[0].dtype),
        grid=(seq_count,),
        in_specs=[pl.BlockSpec((share, width), lambda s: (s, 0))] * 3,
        out_specs=pl.BlockSpec((head_count, share, 3 * chunk_width), lambda s: (s, 0, 0)),
        cost_estimate=pl.CostEstimate(
            flops=0, transcendentals=0, bytes_accessed=2 * 3 * rows_here * head_count * chunk_width * 2
        ),
    )(*xs)


def unpack_kernel(head_count, part_width, chunk_width, *refs):
    o_ref = refs[-1]
    for c, b_ref in enumerate(refs[:-1]):
        for h in range(head_count):
            base = h * part_width + c * chunk_width
            o_ref[:, base : base + chunk_width] = b_ref[h]


def unpack(backs, seq_count, head_count, share, width):
    devices, _, chunk_width = backs[0].shape
    part_width = width // head_count
    return pl.pallas_call(
        functools.partial(unpack_kernel, head_count, part_width, chunk_width),
        out_shape=jax.ShapeDtypeStruct((seq_count * share, width), backs[0].dtype),
        grid=(seq_count,),
        in_specs=[pl.BlockSpec((head_count, share, chunk_width), lambda s: (s, 0, 0))] * len(backs),
        out_specs=pl.BlockSpec((share, width), lambda s: (s, 0)),
        cost_estimate=pl.CostEstimate(
            flops=0, transcendentals=0, bytes_accessed=2 * seq_count * share * width * 2
        ),
    )(*backs)


def body(pos_of_owner, query, key, value, raster_to_tile, window_list, valid_count):
    seq_count = lax.axis_size("seq")
    head_count = lax.axis_size("head")
    seq_pos = lax.axis_index("seq")
    rows_here, width = query.shape
    part_width = width // head_count
    tile_dev, win = window_list.shape
    tok_dev = rows_here * head_count
    tile = tok_dev // tile_dev
    share = rows_here // seq_count
    reach = win - 1
    rim = reach * tile
    ext_tiles = tile_dev + 2 * reach
    heads_here = part_width // HEAD_DIM
    all_tiles = valid_count.shape[0]
    chunks = 2 if heads_here % 2 == 0 else 1
    chunk_heads = heads_here // chunks
    chunk_width = chunk_heads * HEAD_DIM
    devices = seq_count * head_count

    owner_at = [0] * seq_count
    for o, d in enumerate(pos_of_owner):
        owner_at[d] = o
    order = jnp.argsort(raster_to_tile)
    send_order = order.reshape(seq_count, share)[jnp.array(owner_at, jnp.int32)].reshape(rows_here)
    slots_sorted = raster_to_tile[send_order].reshape(seq_count, share)
    slot_send = jnp.broadcast_to(slots_sorted[:, None, :], (seq_count, head_count, share))
    slot_in = lax.all_to_all(
        slot_send.reshape(devices, share), ("seq", "head"), split_axis=0, concat_axis=0, tiled=True
    ).reshape(tok_dev)
    my_owner = jnp.array(owner_at, jnp.int32)[seq_pos]
    local = slot_in - my_owner * tok_dev
    place = jnp.zeros((tok_dev,), jnp.int32).at[local].set(jnp.arange(tok_dev, dtype=jnp.int32))

    window_mine = lax.ppermute(
        window_list, "seq", [(o, pos_of_owner[o]) for o in range(seq_count)]
    )
    first_tile = my_owner * tile_dev - reach
    global_tiles = jnp.clip(first_tile + jnp.arange(ext_tiles, dtype=jnp.int32), 0, all_tiles - 1)
    vc_ext = valid_count[global_tiles]
    local_windows = (window_mine - first_tile).astype(jnp.int32)
    win_flat = local_windows.reshape(tile_dev * win)
    vcw_flat = vc_ext[local_windows].reshape(tile_dev * win)
    vc_own = vc_ext[reach : reach + tile_dev]

    to_right = [(pos_of_owner[o], pos_of_owner[o + 1]) for o in range(seq_count - 1)]
    to_left = [(pos_of_owner[o + 1], pos_of_owner[o]) for o in range(seq_count - 1)]

    packable = share % 16 == 0
    if packable:
        rows_flat = [x[send_order] for x in (query, key, value)]
    else:
        rows_sorted = [
            x[send_order].reshape(seq_count, share, head_count, chunks, chunk_width)
            for x in (query, key, value)
        ]
    arrived = []
    for c in range(chunks):
        if packable:
            send = pack(rows_flat, c, seq_count, head_count, share, chunk_width)
        else:
            send = jnp.concatenate([x[:, :, :, c, :] for x in rows_sorted], axis=3)
            send = jnp.swapaxes(send, 1, 2).reshape(devices, share, 3 * chunk_width)
        got = lax.all_to_all(send, ("seq", "head"), split_axis=0, concat_axis=0, tiled=True)
        got_tile = got.reshape(tok_dev, 3 * chunk_width)[place]
        q_tile = got_tile[:, :chunk_width]
        kv_tile = got_tile[:, chunk_width:]
        from_left = lax.ppermute(kv_tile[tok_dev - rim :], "seq", to_right)
        from_right = lax.ppermute(kv_tile[:rim], "seq", to_left)
        kv_ext = jnp.concatenate([from_left, kv_tile, from_right], axis=0)
        out_tile = attention(q_tile, kv_ext, win_flat, vcw_flat, vc_own, tile, win, chunk_heads)
        outgoing = out_tile[local].reshape(devices, share, chunk_width)
        back = lax.all_to_all(outgoing, ("seq", "head"), split_axis=0, concat_axis=0, tiled=True)
        arrived.append(back)
    if packable:
        sorted_rows = unpack(arrived, seq_count, head_count, share, width)
    else:
        arrived = [b.reshape(seq_count, head_count, share, 1, chunk_width) for b in arrived]
        arrived = jnp.concatenate(arrived, axis=3)
        sorted_rows = jnp.swapaxes(arrived, 1, 2).reshape(rows_here, width)
    inverse = (
        jnp.zeros((rows_here,), jnp.int32).at[send_order].set(jnp.arange(rows_here, dtype=jnp.int32))
    )
    return sorted_rows[inverse]


def snake(mesh):
    seq_count = mesh.shape["seq"]
    first = mesh.devices.reshape(seq_count, -1)[:, 0]
    try:
        spots = [tuple(d.coords) for d in first]
    except AttributeError:
        spots = [(0, d % 2, d // 2) for d in range(seq_count)]
    low_z = min(c[2] for c in spots)

    def rank(d):
        x, y, z = spots[d][:3]
        return (z, y if (z - low_z) % 2 == 0 else -y, x)

    return tuple(sorted(range(seq_count), key=rank))


def solution(mesh):
    placed = (
        P(("seq", "head"), None),
        P(("seq", "head"), None),
        P(("seq", "head"), None),
        P(("seq", "head")),
        P("seq", None),
        P(),
    )
    return jax.shard_map(
        functools.partial(body, snake(mesh)), mesh=mesh, in_specs=placed, out_specs=P(("seq", "head"), None), check_vma=False
    )
```

```python
import functools

import jax
import jax.numpy as jnp
from jax import lax
from jax.experimental import pallas as pl
from jax.experimental.pallas import tpu as pltpu
from jax.sharding import PartitionSpec as P

HEAD_DIM = 128


def attn_kernel(win, tile, scale, win_ref, vcw_ref, vco_ref, q_ref, *refs):
    k_refs = refs[:win]
    v_refs = refs[win : 2 * win]
    o_ref = refs[2 * win]
    s_scr = refs[2 * win + 1]
    i = pl.program_id(0)
    q = q_ref[...]
    col = lax.broadcasted_iota(jnp.int32, (tile, tile), 1)
    for w in range(win):
        s = lax.dot_general(
            q, k_refs[w][...], (((1,), (1,)), ((), ())), preferred_element_type=jnp.float32
        )
        s = s * scale
        s = jnp.where(col < vcw_ref[i * win + w], s, -jnp.inf)
        s_scr[:, w * tile : (w + 1) * tile] = s
    s = s_scr[...]
    m = jnp.max(s, axis=1, keepdims=True)
    p = jnp.exp(s - m)
    total = jnp.sum(p, axis=1, keepdims=True)
    pb = p.astype(jnp.bfloat16)
    acc = jnp.dot(pb[:, 0:tile], v_refs[0][...], preferred_element_type=jnp.float32)
    for w in range(1, win):
        acc = acc + jnp.dot(
            pb[:, w * tile : (w + 1) * tile], v_refs[w][...], preferred_element_type=jnp.float32
        )
    out = acc / total
    row = lax.broadcasted_iota(jnp.int32, (tile, 1), 0)
    out = jnp.where(row < vco_ref[i], out, 0.0)
    o_ref[...] = out.astype(o_ref.dtype)


def attention(q_tile, kv_ext, win_flat, vcw_flat, vc_own, tile, win, heads_here):
    tok_dev, pw = q_tile.shape
    tile_dev = tok_dev // tile
    scale = HEAD_DIM ** (-0.5)

    def q_map(i, j, w_ref, a_ref, b_ref):
        return (i, j)

    def k_map(w, i, j, w_ref, a_ref, b_ref):
        return (w_ref[i * win + w], j)

    def v_map(w, i, j, w_ref, a_ref, b_ref):
        return (w_ref[i * win + w], heads_here + j)

    blk = (tile, HEAD_DIM)
    in_specs = [pl.BlockSpec(blk, q_map)]
    in_specs += [pl.BlockSpec(blk, functools.partial(k_map, w)) for w in range(win)]
    in_specs += [pl.BlockSpec(blk, functools.partial(v_map, w)) for w in range(win)]
    steps = tile_dev * heads_here
    cost = pl.CostEstimate(
        flops=steps * 4 * tile * win * tile * HEAD_DIM,
        transcendentals=steps * tile * win * tile,
        bytes_accessed=steps * (2 * win + 2) * tile * HEAD_DIM * 2,
    )
    return pl.pallas_call(
        functools.partial(attn_kernel, win, tile, scale),
        out_shape=jax.ShapeDtypeStruct((tok_dev, pw), jnp.bfloat16),
        grid_spec=pltpu.PrefetchScalarGridSpec(
            num_scalar_prefetch=3,
            grid=(tile_dev, heads_here),
            in_specs=in_specs,
            out_specs=pl.BlockSpec(blk, q_map),
            scratch_shapes=[pltpu.VMEM((tile, win * tile), jnp.float32)],
        ),
        cost_estimate=cost,
    )(win_flat, vcw_flat, vc_own, q_tile, *([kv_ext] * (2 * win)))


def pack_kernel(head_count, part_width, chunk_width, col0, q_ref, k_ref, v_ref, o_ref):
    for h in range(head_count):
        base = h * part_width + col0
        for t, x_ref in enumerate((q_ref, k_ref, v_ref)):
            o_ref[h, :, t * chunk_width : (t + 1) * chunk_width] = x_ref[:, base : base + chunk_width]


def pack(xs, col0, seq_count, head_count, share, chunk_width):
    rows_here, width = xs[0].shape
    part_width = width // head_count
    return pl.pallas_call(
        functools.partial(pack_kernel, head_count, part_width, chunk_width, col0),
        out_shape=jax.ShapeDtypeStruct((seq_count * head_count, share, 3 * chunk_width), xs[0].dtype),
        grid=(seq_count,),
        in_specs=[pl.BlockSpec((share, width), lambda s: (s, 0))] * 3,
        out_specs=pl.BlockSpec((head_count, share, 3 * chunk_width), lambda s: (s, 0, 0)),
        cost_estimate=pl.CostEstimate(
            flops=0, transcendentals=0, bytes_accessed=2 * 3 * rows_here * head_count * chunk_width * 2
        ),
    )(*xs)


def unpack_kernel(head_count, part_width, spans, *refs):
    o_ref = refs[-1]
    for (col0, chunk_width), b_ref in zip(spans, refs[:-1]):
        for h in range(head_count):
            base = h * part_width + col0
            o_ref[:, base : base + chunk_width] = b_ref[h]


def unpack(backs, seq_count, head_count, share, width):
    part_width = width // head_count
    spans = []
    col0 = 0
    for b in backs:
        spans.append((col0, b.shape[2]))
        col0 += b.shape[2]
    return pl.pallas_call(
        functools.partial(unpack_kernel, head_count, part_width, tuple(spans)),
        out_shape=jax.ShapeDtypeStruct((seq_count * share, width), backs[0].dtype),
        grid=(seq_count,),
        in_specs=[
            pl.BlockSpec((head_count, share, b.shape[2]), lambda s: (s, 0, 0)) for b in backs
        ],
        out_specs=pl.BlockSpec((share, width), lambda s: (s, 0)),
        cost_estimate=pl.CostEstimate(
            flops=0, transcendentals=0, bytes_accessed=2 * seq_count * share * width * 2
        ),
    )(*backs)


def body(pos_of_owner, query, key, value, raster_to_tile, window_list, valid_count):
    seq_count = lax.axis_size("seq")
    head_count = lax.axis_size("head")
    seq_pos = lax.axis_index("seq")
    rows_here, width = query.shape
    part_width = width // head_count
    tile_dev, win = window_list.shape
    tok_dev = rows_here * head_count
    tile = tok_dev // tile_dev
    share = rows_here // seq_count
    reach = win - 1
    rim = reach * tile
    ext_tiles = tile_dev + 2 * reach
    heads_here = part_width // HEAD_DIM
    all_tiles = valid_count.shape[0]
    later = heads_here // 3
    head_split = [heads_here - later, later] if later > 0 else [heads_here]
    devices = seq_count * head_count

    owner_at = [0] * seq_count
    for o, d in enumerate(pos_of_owner):
        owner_at[d] = o
    order = jnp.argsort(raster_to_tile)
    send_order = order.reshape(seq_count, share)[jnp.array(owner_at, jnp.int32)].reshape(rows_here)
    slots_sorted = raster_to_tile[send_order].reshape(seq_count, share)
    slot_send = jnp.broadcast_to(slots_sorted[:, None, :], (seq_count, head_count, share))
    slot_in = lax.all_to_all(
        slot_send.reshape(devices, share), ("seq", "head"), split_axis=0, concat_axis=0, tiled=True
    ).reshape(tok_dev)
    my_owner = jnp.array(owner_at, jnp.int32)[seq_pos]
    local = slot_in - my_owner * tok_dev
    place = jnp.zeros((tok_dev,), jnp.int32).at[local].set(jnp.arange(tok_dev, dtype=jnp.int32))

    window_mine = lax.ppermute(
        window_list, "seq", [(o, pos_of_owner[o]) for o in range(seq_count)]
    )
    first_tile = my_owner * tile_dev - reach
    global_tiles = jnp.clip(first_tile + jnp.arange(ext_tiles, dtype=jnp.int32), 0, all_tiles - 1)
    vc_ext = valid_count[global_tiles]
    local_windows = (window_mine - first_tile).astype(jnp.int32)
    win_flat = local_windows.reshape(tile_dev * win)
    vcw_flat = vc_ext[local_windows].reshape(tile_dev * win)
    vc_own = vc_ext[reach : reach + tile_dev]

    to_right = [(pos_of_owner[o], pos_of_owner[o + 1]) for o in range(seq_count - 1)]
    to_left = [(pos_of_owner[o + 1], pos_of_owner[o]) for o in range(seq_count - 1)]

    packable = share % 16 == 0
    if packable:
        rows_flat = [x[send_order] for x in (query, key, value)]
    else:
        rows_sorted = [
            x[send_order].reshape(seq_count, share, head_count, part_width)
            for x in (query, key, value)
        ]
    arrived = []
    col0 = 0
    for chunk_heads in head_split:
        chunk_width = chunk_heads * HEAD_DIM
        if packable:
            send = pack(rows_flat, col0, seq_count, head_count, share, chunk_width)
        else:
            send = jnp.concatenate(
                [x[:, :, :, col0 : col0 + chunk_width] for x in rows_sorted], axis=3
            )
            send = jnp.swapaxes(send, 1, 2).reshape(devices, share, 3 * chunk_width)
        col0 += chunk_width
        got = lax.all_to_all(send, ("seq", "head"), split_axis=0, concat_axis=0, tiled=True)
        got_tile = got.reshape(tok_dev, 3 * chunk_width)[place]
        q_tile = got_tile[:, :chunk_width]
        kv_tile = got_tile[:, chunk_width:]
        from_left = lax.ppermute(kv_tile[tok_dev - rim :], "seq", to_right)
        from_right = lax.ppermute(kv_tile[:rim], "seq", to_left)
        kv_ext = jnp.concatenate([from_left, kv_tile, from_right], axis=0)
        out_tile = attention(q_tile, kv_ext, win_flat, vcw_flat, vc_own, tile, win, chunk_heads)
        outgoing = out_tile[local].reshape(devices, share, chunk_width)
        back = lax.all_to_all(outgoing, ("seq", "head"), split_axis=0, concat_axis=0, tiled=True)
        arrived.append(back)
    if packable:
        sorted_rows = unpack(arrived, seq_count, head_count, share, width)
    else:
        arrived = [b.reshape(seq_count, head_count, share, b.shape[2]) for b in arrived]
        arrived = jnp.concatenate(arrived, axis=3)
        sorted_rows = jnp.swapaxes(arrived, 1, 2).reshape(rows_here, width)
    inverse = (
        jnp.zeros((rows_here,), jnp.int32).at[send_order].set(jnp.arange(rows_here, dtype=jnp.int32))
    )
    return sorted_rows[inverse]


def snake(mesh):
    seq_count = mesh.shape["seq"]
    first = mesh.devices.reshape(seq_count, -1)[:, 0]
    try:
        spots = [tuple(d.coords) for d in first]
    except AttributeError:
        spots = [(0, d % 2, d // 2) for d in range(seq_count)]
    low_z = min(c[2] for c in spots)

    def rank(d):
        x, y, z = spots[d][:3]
        return (z, y if (z - low_z) % 2 == 0 else -y, x)

    return tuple(sorted(range(seq_count), key=rank))


def solution(mesh):
    placed = (
        P(("seq", "head"), None),
        P(("seq", "head"), None),
        P(("seq", "head"), None),
        P(("seq", "head")),
        P("seq", None),
        P(),
    )
    return jax.shard_map(
        functools.partial(body, snake(mesh)), mesh=mesh, in_specs=placed, out_specs=P(("seq", "head"), None), check_vma=False
    )
```

```python
import functools

import jax
import jax.numpy as jnp
from jax import lax
from jax.experimental import pallas as pl
from jax.experimental.pallas import tpu as pltpu
from jax.sharding import PartitionSpec as P

HEAD_DIM = 128


def attn_kernel(win, tile, scale, win_ref, vcw_ref, vco_ref, q_ref, *refs):
    k_refs = refs[:win]
    v_refs = refs[win : 2 * win]
    o_ref = refs[2 * win]
    i = pl.program_id(0)
    q = q_ref[...]
    col = lax.broadcasted_iota(jnp.int32, (1, tile), 1)
    scores = []
    top = None
    for w in range(win):
        s = lax.dot_general(
            q, k_refs[w][...], (((1,), (1,)), ((), ())), preferred_element_type=jnp.float32
        )
        s = s * scale
        s = jnp.where(col < vcw_ref[i * win + w], s, -jnp.inf)
        scores.append(s)
        m = jnp.max(s, axis=1, keepdims=True)
        top = m if top is None else jnp.maximum(top, m)
    total = None
    acc = None
    for w in range(win):
        p = jnp.exp(scores[w] - top)
        part = jnp.sum(p, axis=1, keepdims=True)
        mix = jnp.dot(p.astype(jnp.bfloat16), v_refs[w][...], preferred_element_type=jnp.float32)
        total = part if total is None else total + part
        acc = mix if acc is None else acc + mix
    out = acc / total
    row = lax.broadcasted_iota(jnp.int32, (tile, 1), 0)
    out = jnp.where(row < vco_ref[i], out, 0.0)
    o_ref[...] = out.astype(o_ref.dtype)


def attention(q_tile, kv_ext, win_flat, vcw_flat, vc_own, tile, win, heads_here):
    tok_dev, pw = q_tile.shape
    tile_dev = tok_dev // tile
    scale = HEAD_DIM ** (-0.5)

    def q_map(i, j, w_ref, a_ref, b_ref):
        return (i, j)

    def k_map(w, i, j, w_ref, a_ref, b_ref):
        return (w_ref[i * win + w], j)

    def v_map(w, i, j, w_ref, a_ref, b_ref):
        return (w_ref[i * win + w], heads_here + j)

    blk = (tile, HEAD_DIM)
    in_specs = [pl.BlockSpec(blk, q_map)]
    in_specs += [pl.BlockSpec(blk, functools.partial(k_map, w)) for w in range(win)]
    in_specs += [pl.BlockSpec(blk, functools.partial(v_map, w)) for w in range(win)]
    steps = tile_dev * heads_here
    cost = pl.CostEstimate(
        flops=steps * 4 * tile * win * tile * HEAD_DIM,
        transcendentals=steps * tile * win * tile,
        bytes_accessed=steps * (2 * win + 2) * tile * HEAD_DIM * 2,
    )
    return pl.pallas_call(
        functools.partial(attn_kernel, win, tile, scale),
        out_shape=jax.ShapeDtypeStruct((tok_dev, pw), jnp.bfloat16),
        grid_spec=pltpu.PrefetchScalarGridSpec(
            num_scalar_prefetch=3,
            grid=(tile_dev, heads_here),
            in_specs=in_specs,
            out_specs=pl.BlockSpec(blk, q_map),
        ),
        cost_estimate=cost,
    )(win_flat, vcw_flat, vc_own, q_tile, *([kv_ext] * (2 * win)))


def pack_kernel(head_count, part_width, chunk_width, c, q_ref, k_ref, v_ref, o_ref):
    for h in range(head_count):
        base = h * part_width + c * chunk_width
        for t, x_ref in enumerate((q_ref, k_ref, v_ref)):
            o_ref[h, :, t * chunk_width : (t + 1) * chunk_width] = x_ref[:, base : base + chunk_width]


def pack(xs, c, seq_count, head_count, share, chunk_width):
    rows_here, width = xs[0].shape
    part_width = width // head_count
    return pl.pallas_call(
        functools.partial(pack_kernel, head_count, part_width, chunk_width, c),
        out_shape=jax.ShapeDtypeStruct((seq_count * head_count, share, 3 * chunk_width), xs[0].dtype),
        grid=(seq_count,),
        in_specs=[pl.BlockSpec((share, width), lambda s: (s, 0))] * 3,
        out_specs=pl.BlockSpec((head_count, share, 3 * chunk_width), lambda s: (s, 0, 0)),
        cost_estimate=pl.CostEstimate(
            flops=0, transcendentals=0, bytes_accessed=2 * 3 * rows_here * head_count * chunk_width * 2
        ),
    )(*xs)


def unpack_kernel(head_count, part_width, chunk_width, *refs):
    o_ref = refs[-1]
    for c, b_ref in enumerate(refs[:-1]):
        for h in range(head_count):
            base = h * part_width + c * chunk_width
            o_ref[:, base : base + chunk_width] = b_ref[h]


def unpack(backs, seq_count, head_count, share, width):
    devices, _, chunk_width = backs[0].shape
    part_width = width // head_count
    return pl.pallas_call(
        functools.partial(unpack_kernel, head_count, part_width, chunk_width),
        out_shape=jax.ShapeDtypeStruct((seq_count * share, width), backs[0].dtype),
        grid=(seq_count,),
        in_specs=[pl.BlockSpec((head_count, share, chunk_width), lambda s: (s, 0, 0))] * len(backs),
        out_specs=pl.BlockSpec((share, width), lambda s: (s, 0)),
        cost_estimate=pl.CostEstimate(
            flops=0, transcendentals=0, bytes_accessed=2 * seq_count * share * width * 2
        ),
    )(*backs)


def body(pos_of_owner, query, key, value, raster_to_tile, window_list, valid_count):
    seq_count = lax.axis_size("seq")
    head_count = lax.axis_size("head")
    seq_pos = lax.axis_index("seq")
    rows_here, width = query.shape
    part_width = width // head_count
    tile_dev, win = window_list.shape
    tok_dev = rows_here * head_count
    tile = tok_dev // tile_dev
    share = rows_here // seq_count
    reach = win - 1
    rim = reach * tile
    ext_tiles = tile_dev + 2 * reach
    heads_here = part_width // HEAD_DIM
    all_tiles = valid_count.shape[0]
    chunks = 2 if heads_here % 2 == 0 else 1
    chunk_heads = heads_here // chunks
    chunk_width = chunk_heads * HEAD_DIM
    devices = seq_count * head_count

    owner_at = [0] * seq_count
    for o, d in enumerate(pos_of_owner):
        owner_at[d] = o
    order = jnp.argsort(raster_to_tile)
    send_order = order.reshape(seq_count, share)[jnp.array(owner_at, jnp.int32)].reshape(rows_here)
    slots_sorted = raster_to_tile[send_order].reshape(seq_count, share)
    slot_send = jnp.broadcast_to(slots_sorted[:, None, :], (seq_count, head_count, share))
    slot_in = lax.all_to_all(
        slot_send.reshape(devices, share), ("seq", "head"), split_axis=0, concat_axis=0, tiled=True
    ).reshape(tok_dev)
    my_owner = jnp.array(owner_at, jnp.int32)[seq_pos]
    local = slot_in - my_owner * tok_dev
    place = jnp.zeros((tok_dev,), jnp.int32).at[local].set(jnp.arange(tok_dev, dtype=jnp.int32))

    window_mine = lax.ppermute(
        window_list, "seq", [(o, pos_of_owner[o]) for o in range(seq_count)]
    )
    first_tile = my_owner * tile_dev - reach
    global_tiles = jnp.clip(first_tile + jnp.arange(ext_tiles, dtype=jnp.int32), 0, all_tiles - 1)
    vc_ext = valid_count[global_tiles]
    local_windows = (window_mine - first_tile).astype(jnp.int32)
    win_flat = local_windows.reshape(tile_dev * win)
    vcw_flat = vc_ext[local_windows].reshape(tile_dev * win)
    vc_own = vc_ext[reach : reach + tile_dev]

    to_right = [(pos_of_owner[o], pos_of_owner[o + 1]) for o in range(seq_count - 1)]
    to_left = [(pos_of_owner[o + 1], pos_of_owner[o]) for o in range(seq_count - 1)]

    packable = share % 16 == 0
    if packable:
        rows_flat = [x[send_order] for x in (query, key, value)]
    else:
        rows_sorted = [
            x[send_order].reshape(seq_count, share, head_count, chunks, chunk_width)
            for x in (query, key, value)
        ]
    arrived = []
    for c in range(chunks):
        if packable:
            send = pack(rows_flat, c, seq_count, head_count, share, chunk_width)
        else:
            send = jnp.concatenate([x[:, :, :, c, :] for x in rows_sorted], axis=3)
            send = jnp.swapaxes(send, 1, 2).reshape(devices, share, 3 * chunk_width)
        got = lax.all_to_all(send, ("seq", "head"), split_axis=0, concat_axis=0, tiled=True)
        got_tile = got.reshape(tok_dev, 3 * chunk_width)[place]
        q_tile = got_tile[:, :chunk_width]
        kv_tile = got_tile[:, chunk_width:]
        from_left = lax.ppermute(kv_tile[tok_dev - rim :], "seq", to_right)
        from_right = lax.ppermute(kv_tile[:rim], "seq", to_left)
        kv_ext = jnp.concatenate([from_left, kv_tile, from_right], axis=0)
        out_tile = attention(q_tile, kv_ext, win_flat, vcw_flat, vc_own, tile, win, chunk_heads)
        outgoing = out_tile[local].reshape(devices, share, chunk_width)
        back = lax.all_to_all(outgoing, ("seq", "head"), split_axis=0, concat_axis=0, tiled=True)
        arrived.append(back)
    if packable:
        sorted_rows = unpack(arrived, seq_count, head_count, share, width)
    else:
        arrived = [b.reshape(seq_count, head_count, share, 1, chunk_width) for b in arrived]
        arrived = jnp.concatenate(arrived, axis=3)
        sorted_rows = jnp.swapaxes(arrived, 1, 2).reshape(rows_here, width)
    inverse = (
        jnp.zeros((rows_here,), jnp.int32).at[send_order].set(jnp.arange(rows_here, dtype=jnp.int32))
    )
    return sorted_rows[inverse]


def snake(mesh):
    seq_count = mesh.shape["seq"]
    first = mesh.devices.reshape(seq_count, -1)[:, 0]
    try:
        spots = [tuple(d.coords) for d in first]
    except AttributeError:
        spots = [(0, d % 2, d // 2) for d in range(seq_count)]
    low_z = min(c[2] for c in spots)

    def rank(d):
        x, y, z = spots[d][:3]
        return (z, y if (z - low_z) % 2 == 0 else -y, x)

    return tuple(sorted(range(seq_count), key=rank))


def solution(mesh):
    placed = (
        P(("seq", "head"), None),
        P(("seq", "head"), None),
        P(("seq", "head"), None),
        P(("seq", "head")),
        P("seq", None),
        P(),
    )
    return jax.shard_map(
        functools.partial(body, snake(mesh)), mesh=mesh, in_specs=placed, out_specs=P(("seq", "head"), None), check_vma=False
    )
```

```python
import functools

import jax
import jax.numpy as jnp
from jax import lax
from jax.experimental import pallas as pl
from jax.experimental.pallas import tpu as pltpu
from jax.sharding import PartitionSpec as P

HEAD_DIM = 128


def attn_kernel(win, tile, scale, win_ref, vcw_ref, vco_ref, q_ref, *refs):
    k_refs = refs[:win]
    v_refs = refs[win : 2 * win]
    o_ref = refs[2 * win]
    i = pl.program_id(0)
    q = q_ref[...]
    col = lax.broadcasted_iota(jnp.int32, (1, tile), 1)
    scores = []
    top = None
    for w in range(win):
        s = lax.dot_general(
            q, k_refs[w][...], (((1,), (1,)), ((), ())), preferred_element_type=jnp.float32
        )
        s = s * scale
        s = jnp.where(col < vcw_ref[i * win + w], s, -jnp.inf)
        scores.append(s)
        m = jnp.max(s, axis=1, keepdims=True)
        top = m if top is None else jnp.maximum(top, m)
    total = None
    acc = None
    for w in range(win):
        p = jnp.exp(scores[w] - top)
        part = jnp.sum(p, axis=1, keepdims=True)
        mix = jnp.dot(p.astype(jnp.bfloat16), v_refs[w][...], preferred_element_type=jnp.float32)
        total = part if total is None else total + part
        acc = mix if acc is None else acc + mix
    out = acc / total
    row = lax.broadcasted_iota(jnp.int32, (tile, 1), 0)
    out = jnp.where(row < vco_ref[i], out, 0.0)
    o_ref[...] = out.astype(o_ref.dtype)


def attention(q_tile, kv_ext, win_flat, vcw_flat, vc_own, tile, win, heads_here):
    tok_dev, pw = q_tile.shape
    tile_dev = tok_dev // tile
    scale = HEAD_DIM ** (-0.5)

    def q_map(i, j, w_ref, a_ref, b_ref):
        return (i, j)

    def k_map(w, i, j, w_ref, a_ref, b_ref):
        return (w_ref[i * win + w], j)

    def v_map(w, i, j, w_ref, a_ref, b_ref):
        return (w_ref[i * win + w], heads_here + j)

    blk = (tile, HEAD_DIM)
    in_specs = [pl.BlockSpec(blk, q_map)]
    in_specs += [pl.BlockSpec(blk, functools.partial(k_map, w)) for w in range(win)]
    in_specs += [pl.BlockSpec(blk, functools.partial(v_map, w)) for w in range(win)]
    steps = tile_dev * heads_here
    cost = pl.CostEstimate(
        flops=steps * 4 * tile * win * tile * HEAD_DIM,
        transcendentals=steps * tile * win * tile,
        bytes_accessed=steps * (2 * win + 2) * tile * HEAD_DIM * 2,
    )
    return pl.pallas_call(
        functools.partial(attn_kernel, win, tile, scale),
        out_shape=jax.ShapeDtypeStruct((tok_dev, pw), jnp.bfloat16),
        grid_spec=pltpu.PrefetchScalarGridSpec(
            num_scalar_prefetch=3,
            grid=(tile_dev, heads_here),
            in_specs=in_specs,
            out_specs=pl.BlockSpec(blk, q_map),
        ),
        cost_estimate=cost,
    )(win_flat, vcw_flat, vc_own, q_tile, *([kv_ext] * (2 * win)))


def pack_kernel(head_count, part_width, chunk_width, c, q_ref, k_ref, v_ref, o_ref):
    for h in range(head_count):
        base = h * part_width + c * chunk_width
        for t, x_ref in enumerate((q_ref, k_ref, v_ref)):
            o_ref[h, :, t * chunk_width : (t + 1) * chunk_width] = x_ref[:, base : base + chunk_width]


def pack(xs, c, seq_count, head_count, share, chunk_width):
    rows_here, width = xs[0].shape
    part_width = width // head_count
    return pl.pallas_call(
        functools.partial(pack_kernel, head_count, part_width, chunk_width, c),
        out_shape=jax.ShapeDtypeStruct((seq_count * head_count, share, 3 * chunk_width), xs[0].dtype),
        grid=(seq_count,),
        in_specs=[pl.BlockSpec((share, width), lambda s: (s, 0))] * 3,
        out_specs=pl.BlockSpec((head_count, share, 3 * chunk_width), lambda s: (s, 0, 0)),
        cost_estimate=pl.CostEstimate(
            flops=0, transcendentals=0, bytes_accessed=2 * 3 * rows_here * head_count * chunk_width * 2
        ),
    )(*xs)


def unpack_kernel(head_count, part_width, chunk_width, *refs):
    o_ref = refs[-1]
    for c, b_ref in enumerate(refs[:-1]):
        for h in range(head_count):
            base = h * part_width + c * chunk_width
            o_ref[:, base : base + chunk_width] = b_ref[h]


def unpack(backs, seq_count, head_count, share, width):
    devices, _, chunk_width = backs[0].shape
    part_width = width // head_count
    return pl.pallas_call(
        functools.partial(unpack_kernel, head_count, part_width, chunk_width),
        out_shape=jax.ShapeDtypeStruct((seq_count * share, width), backs[0].dtype),
        grid=(seq_count,),
        in_specs=[pl.BlockSpec((head_count, share, chunk_width), lambda s: (s, 0, 0))] * len(backs),
        out_specs=pl.BlockSpec((share, width), lambda s: (s, 0)),
        cost_estimate=pl.CostEstimate(
            flops=0, transcendentals=0, bytes_accessed=2 * seq_count * share * width * 2
        ),
    )(*backs)


def body(placements, query, key, value, raster_to_tile, window_list, valid_count):
    seq_count = lax.axis_size("seq")
    head_count = lax.axis_size("head")
    seq_pos = lax.axis_index("seq")
    head_pos = lax.axis_index("head")
    rows_here, width = query.shape
    part_width = width // head_count
    tile_dev, win = window_list.shape
    tok_dev = rows_here * head_count
    tile = tok_dev // tile_dev
    share = rows_here // seq_count
    reach = win - 1
    rim = reach * tile
    ext_tiles = tile_dev + 2 * reach
    heads_here = part_width // HEAD_DIM
    all_tiles = valid_count.shape[0]
    chunks = 2 if heads_here % 2 == 0 else 1
    chunk_heads = heads_here // chunks
    chunk_width = chunk_heads * HEAD_DIM
    devices = seq_count * head_count

    owner_at = [[0] * seq_count for _ in range(head_count)]
    for h in range(head_count):
        for o, d in enumerate(placements[h % len(placements)]):
            owner_at[h][d] = o
    pos_of = [placements[h % len(placements)] for h in range(head_count)]
    send_blocks = [owner_at[h][d] * head_count + h for d in range(seq_count) for h in range(head_count)]
    back_blocks = [pos_of[h][o] * head_count + h for o in range(seq_count) for h in range(head_count)]
    send_blocks = jnp.array(send_blocks, jnp.int32)
    back_blocks = jnp.array(back_blocks, jnp.int32)
    send_order = jnp.argsort(raster_to_tile)
    slots_sorted = raster_to_tile[send_order].reshape(seq_count, share)
    slot_send = jnp.broadcast_to(slots_sorted[:, None, :], (seq_count, head_count, share))
    slot_send = slot_send.reshape(devices, share)[send_blocks]
    slot_in = lax.all_to_all(
        slot_send, ("seq", "head"), split_axis=0, concat_axis=0, tiled=True
    ).reshape(tok_dev)
    my_owner = jnp.array(owner_at, jnp.int32)[head_pos, seq_pos]
    local = slot_in - my_owner * tok_dev
    place = jnp.zeros((tok_dev,), jnp.int32).at[local].set(jnp.arange(tok_dev, dtype=jnp.int32))

    both = ("seq", "head")
    window_mine = lax.ppermute(
        window_list,
        both,
        [(o * head_count + h, pos_of[h][o] * head_count + h) for o in range(seq_count) for h in range(head_count)],
    )
    first_tile = my_owner * tile_dev - reach
    global_tiles = jnp.clip(first_tile + jnp.arange(ext_tiles, dtype=jnp.int32), 0, all_tiles - 1)
    vc_ext = valid_count[global_tiles]
    local_windows = (window_mine - first_tile).astype(jnp.int32)
    win_flat = local_windows.reshape(tile_dev * win)
    vcw_flat = vc_ext[local_windows].reshape(tile_dev * win)
    vc_own = vc_ext[reach : reach + tile_dev]

    to_right = [
        (pos_of[h][o] * head_count + h, pos_of[h][o + 1] * head_count + h)
        for o in range(seq_count - 1)
        for h in range(head_count)
    ]
    to_left = [(b, a) for a, b in to_right]

    packable = share % 16 == 0
    if packable:
        rows_flat = [x[send_order] for x in (query, key, value)]
    else:
        rows_sorted = [
            x[send_order].reshape(seq_count, share, head_count, chunks, chunk_width)
            for x in (query, key, value)
        ]
    arrived = []
    for c in range(chunks):
        if packable:
            send = pack(rows_flat, c, seq_count, head_count, share, chunk_width)
        else:
            send = jnp.concatenate([x[:, :, :, c, :] for x in rows_sorted], axis=3)
            send = jnp.swapaxes(send, 1, 2).reshape(devices, share, 3 * chunk_width)
        got = lax.all_to_all(send[send_blocks], both, split_axis=0, concat_axis=0, tiled=True)
        got_tile = got.reshape(tok_dev, 3 * chunk_width)[place]
        q_tile = got_tile[:, :chunk_width]
        kv_tile = got_tile[:, chunk_width:]
        from_left = lax.ppermute(kv_tile[tok_dev - rim :], both, to_right)
        from_right = lax.ppermute(kv_tile[:rim], both, to_left)
        kv_ext = jnp.concatenate([from_left, kv_tile, from_right], axis=0)
        out_tile = attention(q_tile, kv_ext, win_flat, vcw_flat, vc_own, tile, win, chunk_heads)
        outgoing = out_tile[local].reshape(devices, share, chunk_width)
        back = lax.all_to_all(outgoing, ("seq", "head"), split_axis=0, concat_axis=0, tiled=True)
        arrived.append(back[back_blocks])
    if packable:
        sorted_rows = unpack(arrived, seq_count, head_count, share, width)
    else:
        arrived = [b.reshape(seq_count, head_count, share, 1, chunk_width) for b in arrived]
        arrived = jnp.concatenate(arrived, axis=3)
        sorted_rows = jnp.swapaxes(arrived, 1, 2).reshape(rows_here, width)
    inverse = (
        jnp.zeros((rows_here,), jnp.int32).at[send_order].set(jnp.arange(rows_here, dtype=jnp.int32))
    )
    return sorted_rows[inverse]


def snake(mesh, mirror):
    seq_count = mesh.shape["seq"]
    first = mesh.devices.reshape(seq_count, -1)[:, 0]
    try:
        spots = [tuple(d.coords) for d in first]
    except AttributeError:
        spots = [(0, d % 2, d // 2) for d in range(seq_count)]
    low_z = min(c[2] for c in spots)
    high_y = max(c[1] for c in spots)

    def rank(d):
        x, y, z = spots[d][:3]
        if mirror:
            y = high_y - y
        return (z, y if (z - low_z) % 2 == 0 else -y, x)

    return tuple(sorted(range(seq_count), key=rank))


def solution(mesh):
    placed = (
        P(("seq", "head"), None),
        P(("seq", "head"), None),
        P(("seq", "head"), None),
        P(("seq", "head")),
        P("seq", None),
        P(),
    )
    return jax.shard_map(
        functools.partial(body, (snake(mesh, False), snake(mesh, True))), mesh=mesh, in_specs=placed, out_specs=P(("seq", "head"), None), check_vma=False
    )
```

```python
import functools

import jax
import jax.numpy as jnp
from jax import lax
from jax.experimental import pallas as pl
from jax.experimental.pallas import tpu as pltpu
from jax.sharding import PartitionSpec as P

HEAD_DIM = 128


def attn_kernel(win, tile, scale, win_ref, vcw_ref, vco_ref, q_ref, *refs):
    k_refs = refs[:win]
    v_refs = refs[win : 2 * win]
    o_ref = refs[2 * win]
    i = pl.program_id(0)
    q = q_ref[...]
    col = lax.broadcasted_iota(jnp.int32, (1, tile), 1)
    scores = []
    top = None
    for w in range(win):
        s = lax.dot_general(
            q, k_refs[w][...], (((1,), (1,)), ((), ())), preferred_element_type=jnp.float32
        )
        s = s * scale
        s = jnp.where(col < vcw_ref[i * win + w], s, -jnp.inf)
        scores.append(s)
        m = jnp.max(s, axis=1, keepdims=True)
        top = m if top is None else jnp.maximum(top, m)
    total = None
    acc = None
    for w in range(win):
        p = jnp.exp(scores[w] - top)
        part = jnp.sum(p, axis=1, keepdims=True)
        mix = jnp.dot(p.astype(jnp.bfloat16), v_refs[w][...], preferred_element_type=jnp.float32)
        total = part if total is None else total + part
        acc = mix if acc is None else acc + mix
    out = acc / total
    row = lax.broadcasted_iota(jnp.int32, (tile, 1), 0)
    out = jnp.where(row < vco_ref[i], out, 0.0)
    o_ref[...] = out.astype(o_ref.dtype)


def attention(q_tile, kv_ext, win_flat, vcw_flat, vc_own, tile, win, heads_here):
    tok_dev, pw = q_tile.shape
    tile_dev = tok_dev // tile
    scale = HEAD_DIM ** (-0.5)

    def q_map(i, j, w_ref, a_ref, b_ref):
        return (i, j)

    def k_map(w, i, j, w_ref, a_ref, b_ref):
        return (w_ref[i * win + w], j)

    def v_map(w, i, j, w_ref, a_ref, b_ref):
        return (w_ref[i * win + w], heads_here + j)

    blk = (tile, HEAD_DIM)
    in_specs = [pl.BlockSpec(blk, q_map)]
    in_specs += [pl.BlockSpec(blk, functools.partial(k_map, w)) for w in range(win)]
    in_specs += [pl.BlockSpec(blk, functools.partial(v_map, w)) for w in range(win)]
    steps = tile_dev * heads_here
    cost = pl.CostEstimate(
        flops=steps * 4 * tile * win * tile * HEAD_DIM,
        transcendentals=steps * tile * win * tile,
        bytes_accessed=steps * (2 * win + 2) * tile * HEAD_DIM * 2,
    )
    return pl.pallas_call(
        functools.partial(attn_kernel, win, tile, scale),
        out_shape=jax.ShapeDtypeStruct((tok_dev, pw), jnp.bfloat16),
        grid_spec=pltpu.PrefetchScalarGridSpec(
            num_scalar_prefetch=3,
            grid=(tile_dev, heads_here),
            in_specs=in_specs,
            out_specs=pl.BlockSpec(blk, q_map),
        ),
        cost_estimate=cost,
    )(win_flat, vcw_flat, vc_own, q_tile, *([kv_ext] * (2 * win)))


def pack_kernel(head_count, chunk_width, col0, table_ref, *refs):
    o_ref = refs[-1]
    for h in range(head_count):
        for t in range(3):
            x_ref = refs[t * head_count + h]
            o_ref[h, :, t * chunk_width : (t + 1) * chunk_width] = x_ref[:, col0 : col0 + chunk_width]


def pack(xs, table, col0, seq_count, head_count, share, chunk_width):
    rows_here, width = xs[0].shape
    part_width = width // head_count

    def in_map(h, d, table_ref):
        return (table_ref[d * head_count + h], h)

    in_specs = [
        pl.BlockSpec((share, part_width), functools.partial(in_map, h))
        for t in range(3)
        for h in range(head_count)
    ]
    return pl.pallas_call(
        functools.partial(pack_kernel, head_count, chunk_width, col0),
        out_shape=jax.ShapeDtypeStruct((seq_count * head_count, share, 3 * chunk_width), xs[0].dtype),
        grid_spec=pltpu.PrefetchScalarGridSpec(
            num_scalar_prefetch=1,
            grid=(seq_count,),
            in_specs=in_specs,
            out_specs=pl.BlockSpec((head_count, share, 3 * chunk_width), lambda d, table_ref: (d, 0, 0)),
        ),
        cost_estimate=pl.CostEstimate(
            flops=0, transcendentals=0, bytes_accessed=2 * 3 * rows_here * head_count * chunk_width * 2
        ),
    )(table, *[x for x in xs for h in range(head_count)])


def unpack_kernel(head_count, part_width, chunk_widths, table_ref, *refs):
    o_ref = refs[-1]
    col0 = 0
    for c, chunk_width in enumerate(chunk_widths):
        for h in range(head_count):
            base = h * part_width + col0
            o_ref[:, base : base + chunk_width] = refs[c * head_count + h][0]
        col0 += chunk_width


def unpack(backs, table, seq_count, head_count, share, width):
    part_width = width // head_count

    def in_map(h, o, table_ref):
        return (table_ref[o * head_count + h], 0, 0)

    in_specs = [
        pl.BlockSpec((1, share, b.shape[2]), functools.partial(in_map, h))
        for b in backs
        for h in range(head_count)
    ]
    return pl.pallas_call(
        functools.partial(unpack_kernel, head_count, part_width, tuple(b.shape[2] for b in backs)),
        out_shape=jax.ShapeDtypeStruct((seq_count * share, width), backs[0].dtype),
        grid_spec=pltpu.PrefetchScalarGridSpec(
            num_scalar_prefetch=1,
            grid=(seq_count,),
            in_specs=in_specs,
            out_specs=pl.BlockSpec((share, width), lambda o, table_ref: (o, 0)),
        ),
        cost_estimate=pl.CostEstimate(
            flops=0, transcendentals=0, bytes_accessed=2 * seq_count * share * width * 2
        ),
    )(table, *[b for b in backs for h in range(head_count)])


def body(placements, query, key, value, raster_to_tile, window_list, valid_count):
    seq_count = lax.axis_size("seq")
    head_count = lax.axis_size("head")
    seq_pos = lax.axis_index("seq")
    head_pos = lax.axis_index("head")
    rows_here, width = query.shape
    part_width = width // head_count
    tile_dev, win = window_list.shape
    tok_dev = rows_here * head_count
    tile = tok_dev // tile_dev
    share = rows_here // seq_count
    reach = win - 1
    rim = reach * tile
    ext_tiles = tile_dev + 2 * reach
    heads_here = part_width // HEAD_DIM
    all_tiles = valid_count.shape[0]
    chunks = 2 if heads_here % 2 == 0 else 1
    chunk_heads = heads_here // chunks
    chunk_width = chunk_heads * HEAD_DIM
    devices = seq_count * head_count

    owner_at = [[0] * seq_count for _ in range(head_count)]
    for h in range(head_count):
        for o, d in enumerate(placements[h % len(placements)]):
            owner_at[h][d] = o
    pos_of = [placements[h % len(placements)] for h in range(head_count)]
    send_blocks = [owner_at[h][d] * head_count + h for d in range(seq_count) for h in range(head_count)]
    back_blocks = [pos_of[h][o] * head_count + h for o in range(seq_count) for h in range(head_count)]
    owner_rows = jnp.array(
        [owner_at[h][d] for d in range(seq_count) for h in range(head_count)], jnp.int32
    )
    send_blocks = jnp.array(send_blocks, jnp.int32)
    back_blocks = jnp.array(back_blocks, jnp.int32)
    send_order = jnp.argsort(raster_to_tile)
    slots_sorted = raster_to_tile[send_order].reshape(seq_count, share)
    slot_send = jnp.broadcast_to(slots_sorted[:, None, :], (seq_count, head_count, share))
    slot_send = slot_send.reshape(devices, share)[send_blocks]
    slot_in = lax.all_to_all(
        slot_send, ("seq", "head"), split_axis=0, concat_axis=0, tiled=True
    ).reshape(tok_dev)
    my_owner = jnp.array(owner_at, jnp.int32)[head_pos, seq_pos]
    local = slot_in - my_owner * tok_dev
    place = jnp.zeros((tok_dev,), jnp.int32).at[local].set(jnp.arange(tok_dev, dtype=jnp.int32))

    both = ("seq", "head")
    window_mine = lax.ppermute(
        window_list,
        both,
        [(o * head_count + h, pos_of[h][o] * head_count + h) for o in range(seq_count) for h in range(head_count)],
    )
    first_tile = my_owner * tile_dev - reach
    global_tiles = jnp.clip(first_tile + jnp.arange(ext_tiles, dtype=jnp.int32), 0, all_tiles - 1)
    vc_ext = valid_count[global_tiles]
    local_windows = (window_mine - first_tile).astype(jnp.int32)
    win_flat = local_windows.reshape(tile_dev * win)
    vcw_flat = vc_ext[local_windows].reshape(tile_dev * win)
    vc_own = vc_ext[reach : reach + tile_dev]

    to_right = [
        (pos_of[h][o] * head_count + h, pos_of[h][o + 1] * head_count + h)
        for o in range(seq_count - 1)
        for h in range(head_count)
    ]
    to_left = [(b, a) for a, b in to_right]

    packable = share % 16 == 0
    if packable:
        rows_flat = [x[send_order] for x in (query, key, value)]
    else:
        rows_sorted = [
            x[send_order].reshape(seq_count, share, head_count, chunks, chunk_width)
            for x in (query, key, value)
        ]
    arrived = []
    for c in range(chunks):
        if packable:
            send = pack(rows_flat, owner_rows, c * chunk_width, seq_count, head_count, share, chunk_width)
        else:
            send = jnp.concatenate([x[:, :, :, c, :] for x in rows_sorted], axis=3)
            send = jnp.swapaxes(send, 1, 2).reshape(devices, share, 3 * chunk_width)[send_blocks]
        got = lax.all_to_all(send, both, split_axis=0, concat_axis=0, tiled=True)
        got_tile = got.reshape(tok_dev, 3 * chunk_width)[place]
        q_tile = got_tile[:, :chunk_width]
        kv_tile = got_tile[:, chunk_width:]
        from_left = lax.ppermute(kv_tile[tok_dev - rim :], both, to_right)
        from_right = lax.ppermute(kv_tile[:rim], both, to_left)
        kv_ext = jnp.concatenate([from_left, kv_tile, from_right], axis=0)
        out_tile = attention(q_tile, kv_ext, win_flat, vcw_flat, vc_own, tile, win, chunk_heads)
        outgoing = out_tile[local].reshape(devices, share, chunk_width)
        back = lax.all_to_all(outgoing, ("seq", "head"), split_axis=0, concat_axis=0, tiled=True)
        arrived.append(back)
    if packable:
        sorted_rows = unpack(arrived, back_blocks, seq_count, head_count, share, width)
    else:
        arrived = [b[back_blocks] for b in arrived]
        arrived = [b.reshape(seq_count, head_count, share, 1, chunk_width) for b in arrived]
        arrived = jnp.concatenate(arrived, axis=3)
        sorted_rows = jnp.swapaxes(arrived, 1, 2).reshape(rows_here, width)
    inverse = (
        jnp.zeros((rows_here,), jnp.int32).at[send_order].set(jnp.arange(rows_here, dtype=jnp.int32))
    )
    return sorted_rows[inverse]


def snake(mesh, mirror):
    seq_count = mesh.shape["seq"]
    first = mesh.devices.reshape(seq_count, -1)[:, 0]
    try:
        spots = [tuple(d.coords) for d in first]
    except AttributeError:
        spots = [(0, d % 2, d // 2) for d in range(seq_count)]
    low_z = min(c[2] for c in spots)
    high_y = max(c[1] for c in spots)

    def rank(d):
        x, y, z = spots[d][:3]
        if mirror:
            y = high_y - y
        return (z, y if (z - low_z) % 2 == 0 else -y, x)

    return tuple(sorted(range(seq_count), key=rank))


def solution(mesh):
    placed = (
        P(("seq", "head"), None),
        P(("seq", "head"), None),
        P(("seq", "head"), None),
        P(("seq", "head")),
        P("seq", None),
        P(),
    )
    return jax.shard_map(
        functools.partial(body, (snake(mesh, False), snake(mesh, True))), mesh=mesh, in_specs=placed, out_specs=P(("seq", "head"), None), check_vma=False
    )
```

```python
import functools

import jax
import jax.numpy as jnp
from jax import lax
from jax.experimental import pallas as pl
from jax.experimental.pallas import tpu as pltpu
from jax.sharding import PartitionSpec as P

HEAD_DIM = 128


def attn_kernel(win, tile, scale, heads, win_ref, vcw_ref, vco_ref, q_ref, *refs):
    k_refs = refs[:win]
    v_refs = refs[win : 2 * win]
    o_ref = refs[2 * win]
    i = pl.program_id(0)
    col = lax.broadcasted_iota(jnp.int32, (1, tile), 1)
    row = lax.broadcasted_iota(jnp.int32, (tile, 1), 0)
    for hh in range(heads):
        cols = slice(hh * HEAD_DIM, (hh + 1) * HEAD_DIM)
        q = q_ref[:, cols]
        scores = []
        top = None
        for w in range(win):
            s = lax.dot_general(
                q, k_refs[w][:, cols], (((1,), (1,)), ((), ())), preferred_element_type=jnp.float32
            )
            s = s * scale
            s = jnp.where(col < vcw_ref[i * win + w], s, -jnp.inf)
            scores.append(s)
            m = jnp.max(s, axis=1, keepdims=True)
            top = m if top is None else jnp.maximum(top, m)
        total = None
        acc = None
        for w in range(win):
            p = jnp.exp(scores[w] - top)
            part = jnp.sum(p, axis=1, keepdims=True)
            mix = jnp.dot(
                p.astype(jnp.bfloat16), v_refs[w][:, cols], preferred_element_type=jnp.float32
            )
            total = part if total is None else total + part
            acc = mix if acc is None else acc + mix
        out = acc / total
        out = jnp.where(row < vco_ref[i], out, 0.0)
        o_ref[:, cols] = out.astype(o_ref.dtype)


def attention(q_tile, kv_ext, win_flat, vcw_flat, vc_own, tile, win, heads_here):
    tok_dev, pw = q_tile.shape
    tile_dev = tok_dev // tile
    scale = HEAD_DIM ** (-0.5)

    def q_map(i, w_ref, a_ref, b_ref):
        return (i, 0)

    def k_map(w, i, w_ref, a_ref, b_ref):
        return (w_ref[i * win + w], 0)

    def v_map(w, i, w_ref, a_ref, b_ref):
        return (w_ref[i * win + w], 1)

    blk = (tile, pw)
    in_specs = [pl.BlockSpec(blk, q_map)]
    in_specs += [pl.BlockSpec(blk, functools.partial(k_map, w)) for w in range(win)]
    in_specs += [pl.BlockSpec(blk, functools.partial(v_map, w)) for w in range(win)]
    steps = tile_dev * heads_here
    cost = pl.CostEstimate(
        flops=steps * 4 * tile * win * tile * HEAD_DIM,
        transcendentals=steps * tile * win * tile,
        bytes_accessed=steps * (2 * win + 2) * tile * HEAD_DIM * 2,
    )
    return pl.pallas_call(
        functools.partial(attn_kernel, win, tile, scale, heads_here),
        out_shape=jax.ShapeDtypeStruct((tok_dev, pw), jnp.bfloat16),
        grid_spec=pltpu.PrefetchScalarGridSpec(
            num_scalar_prefetch=3,
            grid=(tile_dev,),
            in_specs=in_specs,
            out_specs=pl.BlockSpec(blk, q_map),
        ),
        cost_estimate=cost,
    )(win_flat, vcw_flat, vc_own, q_tile, *([kv_ext] * (2 * win)))


def pack_kernel(head_count, chunk_width, col0, table_ref, *refs):
    o_ref = refs[-1]
    for h in range(head_count):
        for t in range(3):
            x_ref = refs[t * head_count + h]
            o_ref[h, :, t * chunk_width : (t + 1) * chunk_width] = x_ref[:, col0 : col0 + chunk_width]


def pack(xs, table, col0, seq_count, head_count, share, chunk_width):
    rows_here, width = xs[0].shape
    part_width = width // head_count

    def in_map(h, d, table_ref):
        return (table_ref[d * head_count + h], h)

    in_specs = [
        pl.BlockSpec((share, part_width), functools.partial(in_map, h))
        for t in range(3)
        for h in range(head_count)
    ]
    return pl.pallas_call(
        functools.partial(pack_kernel, head_count, chunk_width, col0),
        out_shape=jax.ShapeDtypeStruct((seq_count * head_count, share, 3 * chunk_width), xs[0].dtype),
        grid_spec=pltpu.PrefetchScalarGridSpec(
            num_scalar_prefetch=1,
            grid=(seq_count,),
            in_specs=in_specs,
            out_specs=pl.BlockSpec((head_count, share, 3 * chunk_width), lambda d, table_ref: (d, 0, 0)),
        ),
        cost_estimate=pl.CostEstimate(
            flops=0, transcendentals=0, bytes_accessed=2 * 3 * rows_here * head_count * chunk_width * 2
        ),
    )(table, *[x for x in xs for h in range(head_count)])


def unpack_kernel(head_count, part_width, chunk_widths, table_ref, *refs):
    o_ref = refs[-1]
    col0 = 0
    for c, chunk_width in enumerate(chunk_widths):
        for h in range(head_count):
            base = h * part_width + col0
            o_ref[:, base : base + chunk_width] = refs[c * head_count + h][0]
        col0 += chunk_width


def unpack(backs, table, seq_count, head_count, share, width):
    part_width = width // head_count

    def in_map(h, o, table_ref):
        return (table_ref[o * head_count + h], 0, 0)

    in_specs = [
        pl.BlockSpec((1, share, b.shape[2]), functools.partial(in_map, h))
        for b in backs
        for h in range(head_count)
    ]
    return pl.pallas_call(
        functools.partial(unpack_kernel, head_count, part_width, tuple(b.shape[2] for b in backs)),
        out_shape=jax.ShapeDtypeStruct((seq_count * share, width), backs[0].dtype),
        grid_spec=pltpu.PrefetchScalarGridSpec(
            num_scalar_prefetch=1,
            grid=(seq_count,),
            in_specs=in_specs,
            out_specs=pl.BlockSpec((share, width), lambda o, table_ref: (o, 0)),
        ),
        cost_estimate=pl.CostEstimate(
            flops=0, transcendentals=0, bytes_accessed=2 * seq_count * share * width * 2
        ),
    )(table, *[b for b in backs for h in range(head_count)])


def body(placements, query, key, value, raster_to_tile, window_list, valid_count):
    seq_count = lax.axis_size("seq")
    head_count = lax.axis_size("head")
    seq_pos = lax.axis_index("seq")
    head_pos = lax.axis_index("head")
    rows_here, width = query.shape
    part_width = width // head_count
    tile_dev, win = window_list.shape
    tok_dev = rows_here * head_count
    tile = tok_dev // tile_dev
    share = rows_here // seq_count
    reach = win - 1
    rim = reach * tile
    ext_tiles = tile_dev + 2 * reach
    heads_here = part_width // HEAD_DIM
    all_tiles = valid_count.shape[0]
    chunks = 2 if heads_here % 2 == 0 else 1
    chunk_heads = heads_here // chunks
    chunk_width = chunk_heads * HEAD_DIM
    devices = seq_count * head_count

    owner_at = [[0] * seq_count for _ in range(head_count)]
    for h in range(head_count):
        for o, d in enumerate(placements[h % len(placements)]):
            owner_at[h][d] = o
    pos_of = [placements[h % len(placements)] for h in range(head_count)]
    send_blocks = [owner_at[h][d] * head_count + h for d in range(seq_count) for h in range(head_count)]
    back_blocks = [pos_of[h][o] * head_count + h for o in range(seq_count) for h in range(head_count)]
    owner_rows = jnp.array(
        [owner_at[h][d] for d in range(seq_count) for h in range(head_count)], jnp.int32
    )
    send_blocks = jnp.array(send_blocks, jnp.int32)
    back_blocks = jnp.array(back_blocks, jnp.int32)
    send_order = jnp.argsort(raster_to_tile)
    slots_sorted = raster_to_tile[send_order].reshape(seq_count, share)
    slot_send = jnp.broadcast_to(slots_sorted[:, None, :], (seq_count, head_count, share))
    slot_send = slot_send.reshape(devices, share)[send_blocks]
    slot_in = lax.all_to_all(
        slot_send, ("seq", "head"), split_axis=0, concat_axis=0, tiled=True
    ).reshape(tok_dev)
    my_owner = jnp.array(owner_at, jnp.int32)[head_pos, seq_pos]
    local = slot_in - my_owner * tok_dev
    place = jnp.zeros((tok_dev,), jnp.int32).at[local].set(jnp.arange(tok_dev, dtype=jnp.int32))

    both = ("seq", "head")
    window_mine = lax.ppermute(
        window_list,
        both,
        [(o * head_count + h, pos_of[h][o] * head_count + h) for o in range(seq_count) for h in range(head_count)],
    )
    first_tile = my_owner * tile_dev - reach
    global_tiles = jnp.clip(first_tile + jnp.arange(ext_tiles, dtype=jnp.int32), 0, all_tiles - 1)
    vc_ext = valid_count[global_tiles]
    local_windows = (window_mine - first_tile).astype(jnp.int32)
    win_flat = local_windows.reshape(tile_dev * win)
    vcw_flat = vc_ext[local_windows].reshape(tile_dev * win)
    vc_own = vc_ext[reach : reach + tile_dev]

    to_right = [
        (pos_of[h][o] * head_count + h, pos_of[h][o + 1] * head_count + h)
        for o in range(seq_count - 1)
        for h in range(head_count)
    ]
    to_left = [(b, a) for a, b in to_right]

    packable = share % 16 == 0
    if packable:
        rows_flat = [x[send_order] for x in (query, key, value)]
    else:
        rows_sorted = [
            x[send_order].reshape(seq_count, share, head_count, chunks, chunk_width)
            for x in (query, key, value)
        ]
    arrived = []
    for c in range(chunks):
        if packable:
            send = pack(rows_flat, owner_rows, c * chunk_width, seq_count, head_count, share, chunk_width)
        else:
            send = jnp.concatenate([x[:, :, :, c, :] for x in rows_sorted], axis=3)
            send = jnp.swapaxes(send, 1, 2).reshape(devices, share, 3 * chunk_width)[send_blocks]
        got = lax.all_to_all(send, both, split_axis=0, concat_axis=0, tiled=True)
        got_tile = got.reshape(tok_dev, 3 * chunk_width)[place]
        q_tile = got_tile[:, :chunk_width]
        kv_tile = got_tile[:, chunk_width:]
        from_left = lax.ppermute(kv_tile[tok_dev - rim :], both, to_right)
        from_right = lax.ppermute(kv_tile[:rim], both, to_left)
        kv_ext = jnp.concatenate([from_left, kv_tile, from_right], axis=0)
        out_tile = attention(q_tile, kv_ext, win_flat, vcw_flat, vc_own, tile, win, chunk_heads)
        outgoing = out_tile[local].reshape(devices, share, chunk_width)
        back = lax.all_to_all(outgoing, ("seq", "head"), split_axis=0, concat_axis=0, tiled=True)
        arrived.append(back)
    if packable:
        sorted_rows = unpack(arrived, back_blocks, seq_count, head_count, share, width)
    else:
        arrived = [b[back_blocks] for b in arrived]
        arrived = [b.reshape(seq_count, head_count, share, 1, chunk_width) for b in arrived]
        arrived = jnp.concatenate(arrived, axis=3)
        sorted_rows = jnp.swapaxes(arrived, 1, 2).reshape(rows_here, width)
    inverse = (
        jnp.zeros((rows_here,), jnp.int32).at[send_order].set(jnp.arange(rows_here, dtype=jnp.int32))
    )
    return sorted_rows[inverse]


def snake(mesh, mirror):
    seq_count = mesh.shape["seq"]
    first = mesh.devices.reshape(seq_count, -1)[:, 0]
    try:
        spots = [tuple(d.coords) for d in first]
    except AttributeError:
        spots = [(0, d % 2, d // 2) for d in range(seq_count)]
    low_z = min(c[2] for c in spots)
    high_y = max(c[1] for c in spots)

    def rank(d):
        x, y, z = spots[d][:3]
        if mirror:
            y = high_y - y
        return (z, y if (z - low_z) % 2 == 0 else -y, x)

    return tuple(sorted(range(seq_count), key=rank))


def solution(mesh):
    placed = (
        P(("seq", "head"), None),
        P(("seq", "head"), None),
        P(("seq", "head"), None),
        P(("seq", "head")),
        P("seq", None),
        P(),
    )
    return jax.shard_map(
        functools.partial(body, (snake(mesh, False), snake(mesh, True))), mesh=mesh, in_specs=placed, out_specs=P(("seq", "head"), None), check_vma=False
    )
```

```python
import functools

import jax
import jax.numpy as jnp
from jax import lax
from jax.experimental import pallas as pl
from jax.experimental.pallas import tpu as pltpu
from jax.sharding import PartitionSpec as P

HEAD_DIM = 128


def attn_kernel(win, tile, scale, heads, win_ref, vcw_ref, vco_ref, q_ref, *refs):
    k_refs = refs[:win]
    v_refs = refs[win : 2 * win]
    o_ref = refs[2 * win]
    i = pl.program_id(0)
    col = lax.broadcasted_iota(jnp.int32, (1, tile), 1)
    row = lax.broadcasted_iota(jnp.int32, (tile, 1), 0)
    for hh in range(heads):
        cols = slice(hh * HEAD_DIM, (hh + 1) * HEAD_DIM)
        q = q_ref[:, cols]
        scores = []
        top = None
        for w in range(win):
            s = lax.dot_general(
                q, k_refs[w][:, cols], (((1,), (1,)), ((), ())), preferred_element_type=jnp.float32
            )
            s = s * scale
            s = jnp.where(col < vcw_ref[i * win + w], s, -jnp.inf)
            scores.append(s)
            m = jnp.max(s, axis=1, keepdims=True)
            top = m if top is None else jnp.maximum(top, m)
        total = None
        acc = None
        for w in range(win):
            p = jnp.exp(scores[w] - top)
            part = jnp.sum(p, axis=1, keepdims=True)
            mix = jnp.dot(
                p.astype(jnp.bfloat16), v_refs[w][:, cols], preferred_element_type=jnp.float32
            )
            total = part if total is None else total + part
            acc = mix if acc is None else acc + mix
        out = acc / total
        out = jnp.where(row < vco_ref[i], out, 0.0)
        o_ref[:, cols] = out.astype(o_ref.dtype)


def attention(q_tile, kv_ext, win_flat, vcw_flat, vc_own, tile, win, heads_here):
    tok_dev, pw = q_tile.shape
    tile_dev = tok_dev // tile
    scale = HEAD_DIM ** (-0.5)

    def q_map(i, w_ref, a_ref, b_ref):
        return (i, 0)

    def k_map(w, i, w_ref, a_ref, b_ref):
        return (w_ref[i * win + w], 0)

    def v_map(w, i, w_ref, a_ref, b_ref):
        return (w_ref[i * win + w], 1)

    blk = (tile, pw)
    in_specs = [pl.BlockSpec(blk, q_map)]
    in_specs += [pl.BlockSpec(blk, functools.partial(k_map, w)) for w in range(win)]
    in_specs += [pl.BlockSpec(blk, functools.partial(v_map, w)) for w in range(win)]
    steps = tile_dev * heads_here
    cost = pl.CostEstimate(
        flops=steps * 4 * tile * win * tile * HEAD_DIM,
        transcendentals=steps * tile * win * tile,
        bytes_accessed=steps * (2 * win + 2) * tile * HEAD_DIM * 2,
    )
    return pl.pallas_call(
        functools.partial(attn_kernel, win, tile, scale, heads_here),
        out_shape=jax.ShapeDtypeStruct((tok_dev, pw), jnp.bfloat16),
        grid_spec=pltpu.PrefetchScalarGridSpec(
            num_scalar_prefetch=3,
            grid=(tile_dev,),
            in_specs=in_specs,
            out_specs=pl.BlockSpec(blk, q_map),
        ),
        cost_estimate=cost,
    )(win_flat, vcw_flat, vc_own, q_tile, *([kv_ext] * (2 * win)))


def pack_kernel(head_count, chunk_width, col0, table_ref, *refs):
    o_ref = refs[-1]
    for h in range(head_count):
        for t in range(3):
            x_ref = refs[t * head_count + h]
            o_ref[h, :, t * chunk_width : (t + 1) * chunk_width] = x_ref[:, col0 : col0 + chunk_width]


def pack(xs, table, col0, seq_count, head_count, share, chunk_width):
    rows_here, width = xs[0].shape
    part_width = width // head_count

    def in_map(h, d, table_ref):
        return (table_ref[d * head_count + h], h)

    in_specs = [
        pl.BlockSpec((share, part_width), functools.partial(in_map, h))
        for t in range(3)
        for h in range(head_count)
    ]
    return pl.pallas_call(
        functools.partial(pack_kernel, head_count, chunk_width, col0),
        out_shape=jax.ShapeDtypeStruct((seq_count * head_count, share, 3 * chunk_width), xs[0].dtype),
        grid_spec=pltpu.PrefetchScalarGridSpec(
            num_scalar_prefetch=1,
            grid=(seq_count,),
            in_specs=in_specs,
            out_specs=pl.BlockSpec((head_count, share, 3 * chunk_width), lambda d, table_ref: (d, 0, 0)),
        ),
        cost_estimate=pl.CostEstimate(
            flops=0, transcendentals=0, bytes_accessed=2 * 3 * rows_here * head_count * chunk_width * 2
        ),
    )(table, *[x for x in xs for h in range(head_count)])


def unpack_kernel(head_count, part_width, chunk_widths, table_ref, *refs):
    o_ref = refs[-1]
    col0 = 0
    for c, chunk_width in enumerate(chunk_widths):
        for h in range(head_count):
            base = h * part_width + col0
            o_ref[:, base : base + chunk_width] = refs[c * head_count + h][0]
        col0 += chunk_width


def unpack(backs, table, seq_count, head_count, share, width):
    part_width = width // head_count

    def in_map(h, o, table_ref):
        return (table_ref[o * head_count + h], 0, 0)

    in_specs = [
        pl.BlockSpec((1, share, b.shape[2]), functools.partial(in_map, h))
        for b in backs
        for h in range(head_count)
    ]
    return pl.pallas_call(
        functools.partial(unpack_kernel, head_count, part_width, tuple(b.shape[2] for b in backs)),
        out_shape=jax.ShapeDtypeStruct((seq_count * share, width), backs[0].dtype),
        grid_spec=pltpu.PrefetchScalarGridSpec(
            num_scalar_prefetch=1,
            grid=(seq_count,),
            in_specs=in_specs,
            out_specs=pl.BlockSpec((share, width), lambda o, table_ref: (o, 0)),
        ),
        cost_estimate=pl.CostEstimate(
            flops=0, transcendentals=0, bytes_accessed=2 * seq_count * share * width * 2
        ),
    )(table, *[b for b in backs for h in range(head_count)])


def body(placements, query, key, value, raster_to_tile, window_list, valid_count):
    seq_count = lax.axis_size("seq")
    head_count = lax.axis_size("head")
    seq_pos = lax.axis_index("seq")
    head_pos = lax.axis_index("head")
    rows_here, width = query.shape
    part_width = width // head_count
    tile_dev, win = window_list.shape
    tok_dev = rows_here * head_count
    tile = tok_dev // tile_dev
    share = rows_here // seq_count
    reach = win - 1
    rim = reach * tile
    ext_tiles = tile_dev + 2 * reach
    heads_here = part_width // HEAD_DIM
    all_tiles = valid_count.shape[0]
    chunks = 2 if heads_here % 2 == 0 else 1
    chunk_heads = heads_here // chunks
    chunk_width = chunk_heads * HEAD_DIM
    devices = seq_count * head_count

    owner_at = [[0] * seq_count for _ in range(head_count)]
    for h in range(head_count):
        for o, d in enumerate(placements[h % len(placements)]):
            owner_at[h][d] = o
    pos_of = [placements[h % len(placements)] for h in range(head_count)]
    send_blocks = [owner_at[h][d] * head_count + h for d in range(seq_count) for h in range(head_count)]
    back_blocks = [pos_of[h][o] * head_count + h for o in range(seq_count) for h in range(head_count)]
    owner_rows = jnp.array(
        [owner_at[h][d] for d in range(seq_count) for h in range(head_count)], jnp.int32
    )
    send_blocks = jnp.array(send_blocks, jnp.int32)
    back_blocks = jnp.array(back_blocks, jnp.int32)
    send_order = jnp.argsort(raster_to_tile)
    slots_sorted = raster_to_tile[send_order].reshape(seq_count, share)
    slot_send = jnp.broadcast_to(slots_sorted[:, None, :], (seq_count, head_count, share))
    slot_send = slot_send.reshape(devices, share)[send_blocks]
    slot_in = lax.all_to_all(
        slot_send, ("seq", "head"), split_axis=0, concat_axis=0, tiled=True
    ).reshape(tok_dev)
    my_owner = jnp.array(owner_at, jnp.int32)[head_pos, seq_pos]
    local = slot_in - my_owner * tok_dev
    place = jnp.zeros((tok_dev,), jnp.int32).at[local].set(jnp.arange(tok_dev, dtype=jnp.int32))

    both = ("seq", "head")
    window_mine = lax.ppermute(
        window_list,
        both,
        [(o * head_count + h, pos_of[h][o] * head_count + h) for o in range(seq_count) for h in range(head_count)],
    )
    first_tile = my_owner * tile_dev - reach
    global_tiles = jnp.clip(first_tile + jnp.arange(ext_tiles, dtype=jnp.int32), 0, all_tiles - 1)
    vc_ext = valid_count[global_tiles]
    local_windows = (window_mine - first_tile).astype(jnp.int32)
    win_flat = local_windows.reshape(tile_dev * win)
    vcw_flat = vc_ext[local_windows].reshape(tile_dev * win)
    vc_own = vc_ext[reach : reach + tile_dev]

    to_right = [
        (pos_of[h][o] * head_count + h, pos_of[h][o + 1] * head_count + h)
        for o in range(seq_count - 1)
        for h in range(head_count)
    ]
    to_left = [(b, a) for a, b in to_right]

    packable = share % 16 == 0
    if packable:
        pick = (send_order[:, None] == jnp.arange(rows_here, dtype=jnp.int32)[None, :]).astype(query.dtype)
        rows_flat = [jnp.dot(pick, x) for x in (query, key, value)]
    else:
        rows_sorted = [
            x[send_order].reshape(seq_count, share, head_count, chunks, chunk_width)
            for x in (query, key, value)
        ]
    arrived = []
    for c in range(chunks):
        if packable:
            send = pack(rows_flat, owner_rows, c * chunk_width, seq_count, head_count, share, chunk_width)
        else:
            send = jnp.concatenate([x[:, :, :, c, :] for x in rows_sorted], axis=3)
            send = jnp.swapaxes(send, 1, 2).reshape(devices, share, 3 * chunk_width)[send_blocks]
        got = lax.all_to_all(send, both, split_axis=0, concat_axis=0, tiled=True)
        got_tile = got.reshape(tok_dev, 3 * chunk_width)[place]
        q_tile = got_tile[:, :chunk_width]
        kv_tile = got_tile[:, chunk_width:]
        from_left = lax.ppermute(kv_tile[tok_dev - rim :], both, to_right)
        from_right = lax.ppermute(kv_tile[:rim], both, to_left)
        kv_ext = jnp.concatenate([from_left, kv_tile, from_right], axis=0)
        out_tile = attention(q_tile, kv_ext, win_flat, vcw_flat, vc_own, tile, win, chunk_heads)
        outgoing = out_tile[local].reshape(devices, share, chunk_width)
        back = lax.all_to_all(outgoing, ("seq", "head"), split_axis=0, concat_axis=0, tiled=True)
        arrived.append(back)
    if packable:
        sorted_rows = unpack(arrived, back_blocks, seq_count, head_count, share, width)
    else:
        arrived = [b[back_blocks] for b in arrived]
        arrived = [b.reshape(seq_count, head_count, share, 1, chunk_width) for b in arrived]
        arrived = jnp.concatenate(arrived, axis=3)
        sorted_rows = jnp.swapaxes(arrived, 1, 2).reshape(rows_here, width)
    inverse = (
        jnp.zeros((rows_here,), jnp.int32).at[send_order].set(jnp.arange(rows_here, dtype=jnp.int32))
    )
    if packable:
        return lax.dot_general(pick, sorted_rows, (((0,), (0,)), ((), ())))
    return sorted_rows[inverse]


def snake(mesh, mirror):
    seq_count = mesh.shape["seq"]
    first = mesh.devices.reshape(seq_count, -1)[:, 0]
    try:
        spots = [tuple(d.coords) for d in first]
    except AttributeError:
        spots = [(0, d % 2, d // 2) for d in range(seq_count)]
    low_z = min(c[2] for c in spots)
    high_y = max(c[1] for c in spots)

    def rank(d):
        x, y, z = spots[d][:3]
        if mirror:
            y = high_y - y
        return (z, y if (z - low_z) % 2 == 0 else -y, x)

    return tuple(sorted(range(seq_count), key=rank))


def solution(mesh):
    placed = (
        P(("seq", "head"), None),
        P(("seq", "head"), None),
        P(("seq", "head"), None),
        P(("seq", "head")),
        P("seq", None),
        P(),
    )
    return jax.shard_map(
        functools.partial(body, (snake(mesh, False), snake(mesh, True))), mesh=mesh, in_specs=placed, out_specs=P(("seq", "head"), None), check_vma=False
    )
```

```python
import functools

import jax
import jax.numpy as jnp
from jax import lax
from jax.experimental import pallas as pl
from jax.experimental.pallas import tpu as pltpu
from jax.sharding import PartitionSpec as P

HEAD_DIM = 128


def attn_kernel(win, tile, scale, heads, win_ref, vcw_ref, vco_ref, q_ref, *refs):
    k_refs = refs[:win]
    v_refs = refs[win : 2 * win]
    o_ref = refs[2 * win]
    i = pl.program_id(0)
    col = lax.broadcasted_iota(jnp.int32, (1, tile), 1)
    row = lax.broadcasted_iota(jnp.int32, (tile, 1), 0)
    for hh in range(heads):
        cols = slice(hh * HEAD_DIM, (hh + 1) * HEAD_DIM)
        q = q_ref[:, cols]
        scores = []
        top = None
        for w in range(win):
            s = lax.dot_general(
                q, k_refs[w][:, cols], (((1,), (1,)), ((), ())), preferred_element_type=jnp.float32
            )
            s = s * scale
            s = jnp.where(col < vcw_ref[i * win + w], s, -jnp.inf)
            scores.append(s)
            m = jnp.max(s, axis=1, keepdims=True)
            top = m if top is None else jnp.maximum(top, m)
        total = None
        acc = None
        for w in range(win):
            p = jnp.exp(scores[w] - top)
            part = jnp.sum(p, axis=1, keepdims=True)
            mix = jnp.dot(
                p.astype(jnp.bfloat16), v_refs[w][:, cols], preferred_element_type=jnp.float32
            )
            total = part if total is None else total + part
            acc = mix if acc is None else acc + mix
        out = acc / total
        out = jnp.where(row < vco_ref[i], out, 0.0)
        o_ref[:, cols] = out.astype(o_ref.dtype)


def attention(q_tile, kv_ext, win_flat, vcw_flat, vc_own, tile, win, heads_here):
    tok_dev, pw = q_tile.shape
    tile_dev = tok_dev // tile
    scale = HEAD_DIM ** (-0.5)

    def q_map(i, w_ref, a_ref, b_ref):
        return (i, 0)

    def k_map(w, i, w_ref, a_ref, b_ref):
        return (w_ref[i * win + w], 0)

    def v_map(w, i, w_ref, a_ref, b_ref):
        return (w_ref[i * win + w], 1)

    blk = (tile, pw)
    in_specs = [pl.BlockSpec(blk, q_map)]
    in_specs += [pl.BlockSpec(blk, functools.partial(k_map, w)) for w in range(win)]
    in_specs += [pl.BlockSpec(blk, functools.partial(v_map, w)) for w in range(win)]
    steps = tile_dev * heads_here
    cost = pl.CostEstimate(
        flops=steps * 4 * tile * win * tile * HEAD_DIM,
        transcendentals=steps * tile * win * tile,
        bytes_accessed=steps * (2 * win + 2) * tile * HEAD_DIM * 2,
    )
    return pl.pallas_call(
        functools.partial(attn_kernel, win, tile, scale, heads_here),
        out_shape=jax.ShapeDtypeStruct((tok_dev, pw), jnp.bfloat16),
        grid_spec=pltpu.PrefetchScalarGridSpec(
            num_scalar_prefetch=3,
            grid=(tile_dev,),
            in_specs=in_specs,
            out_specs=pl.BlockSpec(blk, q_map),
        ),
        cost_estimate=cost,
    )(win_flat, vcw_flat, vc_own, q_tile, *([kv_ext] * (2 * win)))


def pack_kernel(head_count, chunk_width, col0, table_ref, *refs):
    o_ref = refs[-1]
    for h in range(head_count):
        for t in range(3):
            x_ref = refs[t * head_count + h]
            o_ref[h, :, t * chunk_width : (t + 1) * chunk_width] = x_ref[:, col0 : col0 + chunk_width]


def pack(xs, table, col0, seq_count, head_count, share, chunk_width):
    rows_here, width = xs[0].shape
    part_width = width // head_count

    def in_map(h, d, table_ref):
        return (table_ref[d * head_count + h], h)

    in_specs = [
        pl.BlockSpec((share, part_width), functools.partial(in_map, h))
        for t in range(3)
        for h in range(head_count)
    ]
    return pl.pallas_call(
        functools.partial(pack_kernel, head_count, chunk_width, col0),
        out_shape=jax.ShapeDtypeStruct((seq_count * head_count, share, 3 * chunk_width), xs[0].dtype),
        grid_spec=pltpu.PrefetchScalarGridSpec(
            num_scalar_prefetch=1,
            grid=(seq_count,),
            in_specs=in_specs,
            out_specs=pl.BlockSpec((head_count, share, 3 * chunk_width), lambda d, table_ref: (d, 0, 0)),
        ),
        cost_estimate=pl.CostEstimate(
            flops=0, transcendentals=0, bytes_accessed=2 * 3 * rows_here * head_count * chunk_width * 2
        ),
    )(table, *[x for x in xs for h in range(head_count)])


def unpack_kernel(head_count, part_width, chunk_widths, table_ref, *refs):
    o_ref = refs[-1]
    col0 = 0
    for c, chunk_width in enumerate(chunk_widths):
        for h in range(head_count):
            base = h * part_width + col0
            o_ref[:, base : base + chunk_width] = refs[c * head_count + h][0]
        col0 += chunk_width


def unpack(backs, table, seq_count, head_count, share, width):
    part_width = width // head_count

    def in_map(h, o, table_ref):
        return (table_ref[o * head_count + h], 0, 0)

    in_specs = [
        pl.BlockSpec((1, share, b.shape[2]), functools.partial(in_map, h))
        for b in backs
        for h in range(head_count)
    ]
    return pl.pallas_call(
        functools.partial(unpack_kernel, head_count, part_width, tuple(b.shape[2] for b in backs)),
        out_shape=jax.ShapeDtypeStruct((seq_count * share, width), backs[0].dtype),
        grid_spec=pltpu.PrefetchScalarGridSpec(
            num_scalar_prefetch=1,
            grid=(seq_count,),
            in_specs=in_specs,
            out_specs=pl.BlockSpec((share, width), lambda o, table_ref: (o, 0)),
        ),
        cost_estimate=pl.CostEstimate(
            flops=0, transcendentals=0, bytes_accessed=2 * seq_count * share * width * 2
        ),
    )(table, *[b for b in backs for h in range(head_count)])


def body(placements, query, key, value, raster_to_tile, window_list, valid_count):
    seq_count = lax.axis_size("seq")
    head_count = lax.axis_size("head")
    seq_pos = lax.axis_index("seq")
    head_pos = lax.axis_index("head")
    rows_here, width = query.shape
    part_width = width // head_count
    tile_dev, win = window_list.shape
    tok_dev = rows_here * head_count
    tile = tok_dev // tile_dev
    share = rows_here // seq_count
    reach = win - 1
    rim = reach * tile
    ext_tiles = tile_dev + 2 * reach
    heads_here = part_width // HEAD_DIM
    all_tiles = valid_count.shape[0]
    chunks = 2 if heads_here % 2 == 0 else 1
    chunk_heads = heads_here // chunks
    chunk_width = chunk_heads * HEAD_DIM
    devices = seq_count * head_count

    owner_at = [[0] * seq_count for _ in range(head_count)]
    for h in range(head_count):
        for o, d in enumerate(placements[h % len(placements)]):
            owner_at[h][d] = o
    pos_of = [placements[h % len(placements)] for h in range(head_count)]
    send_blocks = [owner_at[h][d] * head_count + h for d in range(seq_count) for h in range(head_count)]
    back_blocks = [pos_of[h][o] * head_count + h for o in range(seq_count) for h in range(head_count)]
    owner_rows = jnp.array(
        [owner_at[h][d] for d in range(seq_count) for h in range(head_count)], jnp.int32
    )
    send_blocks = jnp.array(send_blocks, jnp.int32)
    back_blocks = jnp.array(back_blocks, jnp.int32)
    send_order = jnp.argsort(raster_to_tile)
    slots_sorted = raster_to_tile[send_order].reshape(seq_count, share)
    slot_send = jnp.broadcast_to(slots_sorted[:, None, :], (seq_count, head_count, share))
    slot_send = slot_send.reshape(devices, share)[send_blocks]
    slot_in = lax.all_to_all(
        slot_send, ("seq", "head"), split_axis=0, concat_axis=0, tiled=True
    ).reshape(tok_dev)
    my_owner = jnp.array(owner_at, jnp.int32)[head_pos, seq_pos]
    local = slot_in - my_owner * tok_dev
    place = jnp.zeros((tok_dev,), jnp.int32).at[local].set(jnp.arange(tok_dev, dtype=jnp.int32))
    route = (local[:, None] == jnp.arange(tok_dev, dtype=jnp.int32)[None, :]).astype(query.dtype)

    both = ("seq", "head")
    window_mine = lax.ppermute(
        window_list,
        both,
        [(o * head_count + h, pos_of[h][o] * head_count + h) for o in range(seq_count) for h in range(head_count)],
    )
    first_tile = my_owner * tile_dev - reach
    global_tiles = jnp.clip(first_tile + jnp.arange(ext_tiles, dtype=jnp.int32), 0, all_tiles - 1)
    vc_ext = valid_count[global_tiles]
    local_windows = (window_mine - first_tile).astype(jnp.int32)
    win_flat = local_windows.reshape(tile_dev * win)
    vcw_flat = vc_ext[local_windows].reshape(tile_dev * win)
    vc_own = vc_ext[reach : reach + tile_dev]

    to_right = [
        (pos_of[h][o] * head_count + h, pos_of[h][o + 1] * head_count + h)
        for o in range(seq_count - 1)
        for h in range(head_count)
    ]
    to_left = [(b, a) for a, b in to_right]

    packable = share % 16 == 0
    if packable:
        pick = (send_order[:, None] == jnp.arange(rows_here, dtype=jnp.int32)[None, :]).astype(query.dtype)
        rows_flat = [jnp.dot(pick, x) for x in (query, key, value)]
    else:
        rows_sorted = [
            x[send_order].reshape(seq_count, share, head_count, chunks, chunk_width)
            for x in (query, key, value)
        ]
    arrived = []
    for c in range(chunks):
        if packable:
            send = pack(rows_flat, owner_rows, c * chunk_width, seq_count, head_count, share, chunk_width)
        else:
            send = jnp.concatenate([x[:, :, :, c, :] for x in rows_sorted], axis=3)
            send = jnp.swapaxes(send, 1, 2).reshape(devices, share, 3 * chunk_width)[send_blocks]
        got = lax.all_to_all(send, both, split_axis=0, concat_axis=0, tiled=True)
        got_tile = got.reshape(tok_dev, 3 * chunk_width)[place]
        q_tile = got_tile[:, :chunk_width]
        kv_tile = got_tile[:, chunk_width:]
        from_left = lax.ppermute(kv_tile[tok_dev - rim :], both, to_right)
        from_right = lax.ppermute(kv_tile[:rim], both, to_left)
        kv_ext = jnp.concatenate([from_left, kv_tile, from_right], axis=0)
        out_tile = attention(q_tile, kv_ext, win_flat, vcw_flat, vc_own, tile, win, chunk_heads)
        if packable:
            outgoing = jnp.dot(route, out_tile).reshape(devices, share, chunk_width)
        else:
            outgoing = out_tile[local].reshape(devices, share, chunk_width)
        back = lax.all_to_all(outgoing, ("seq", "head"), split_axis=0, concat_axis=0, tiled=True)
        arrived.append(back)
    if packable:
        sorted_rows = unpack(arrived, back_blocks, seq_count, head_count, share, width)
    else:
        arrived = [b[back_blocks] for b in arrived]
        arrived = [b.reshape(seq_count, head_count, share, 1, chunk_width) for b in arrived]
        arrived = jnp.concatenate(arrived, axis=3)
        sorted_rows = jnp.swapaxes(arrived, 1, 2).reshape(rows_here, width)
    inverse = (
        jnp.zeros((rows_here,), jnp.int32).at[send_order].set(jnp.arange(rows_here, dtype=jnp.int32))
    )
    if packable:
        return lax.dot_general(pick, sorted_rows, (((0,), (0,)), ((), ())))
    return sorted_rows[inverse]


def snake(mesh, mirror):
    seq_count = mesh.shape["seq"]
    first = mesh.devices.reshape(seq_count, -1)[:, 0]
    try:
        spots = [tuple(d.coords) for d in first]
    except AttributeError:
        spots = [(0, d % 2, d // 2) for d in range(seq_count)]
    low_z = min(c[2] for c in spots)
    high_y = max(c[1] for c in spots)

    def rank(d):
        x, y, z = spots[d][:3]
        if mirror:
            y = high_y - y
        return (z, y if (z - low_z) % 2 == 0 else -y, x)

    return tuple(sorted(range(seq_count), key=rank))


def solution(mesh):
    placed = (
        P(("seq", "head"), None),
        P(("seq", "head"), None),
        P(("seq", "head"), None),
        P(("seq", "head")),
        P("seq", None),
        P(),
    )
    return jax.shard_map(
        functools.partial(body, (snake(mesh, False), snake(mesh, True))), mesh=mesh, in_specs=placed, out_specs=P(("seq", "head"), None), check_vma=False
    )
```

```python
import functools

import jax
import jax.numpy as jnp
from jax import lax
from jax.experimental import pallas as pl
from jax.experimental.pallas import tpu as pltpu
from jax.sharding import PartitionSpec as P

HEAD_DIM = 128


def attn_kernel(win, tile, scale, heads, win_ref, vcw_ref, vco_ref, q_ref, *refs):
    k_refs = refs[:win]
    v_refs = refs[win : 2 * win]
    o_ref = refs[2 * win]
    i = pl.program_id(0)
    col = lax.broadcasted_iota(jnp.int32, (1, tile), 1)
    row = lax.broadcasted_iota(jnp.int32, (tile, 1), 0)
    for hh in range(heads):
        cols = slice(hh * HEAD_DIM, (hh + 1) * HEAD_DIM)
        q = q_ref[:, cols]
        scores = []
        top = None
        for w in range(win):
            s = lax.dot_general(
                q, k_refs[w][:, cols], (((1,), (1,)), ((), ())), preferred_element_type=jnp.float32
            )
            s = s * scale
            s = jnp.where(col < vcw_ref[i * win + w], s, -jnp.inf)
            scores.append(s)
            m = jnp.max(s, axis=1, keepdims=True)
            top = m if top is None else jnp.maximum(top, m)
        total = None
        acc = None
        for w in range(win):
            p = jnp.exp(scores[w] - top)
            part = jnp.sum(p, axis=1, keepdims=True)
            mix = jnp.dot(
                p.astype(jnp.bfloat16), v_refs[w][:, cols], preferred_element_type=jnp.float32
            )
            total = part if total is None else total + part
            acc = mix if acc is None else acc + mix
        out = acc / total
        out = jnp.where(row < vco_ref[i], out, 0.0)
        o_ref[:, cols] = out.astype(o_ref.dtype)


def attention(q_tile, kv_ext, win_flat, vcw_flat, vc_own, tile, win, heads_here):
    tok_dev, pw = q_tile.shape
    tile_dev = tok_dev // tile
    scale = HEAD_DIM ** (-0.5)

    def q_map(i, w_ref, a_ref, b_ref):
        return (i, 0)

    def k_map(w, i, w_ref, a_ref, b_ref):
        return (w_ref[i * win + w], 0)

    def v_map(w, i, w_ref, a_ref, b_ref):
        return (w_ref[i * win + w], 1)

    blk = (tile, pw)
    in_specs = [pl.BlockSpec(blk, q_map)]
    in_specs += [pl.BlockSpec(blk, functools.partial(k_map, w)) for w in range(win)]
    in_specs += [pl.BlockSpec(blk, functools.partial(v_map, w)) for w in range(win)]
    steps = tile_dev * heads_here
    cost = pl.CostEstimate(
        flops=steps * 4 * tile * win * tile * HEAD_DIM,
        transcendentals=steps * tile * win * tile,
        bytes_accessed=steps * (2 * win + 2) * tile * HEAD_DIM * 2,
    )
    return pl.pallas_call(
        functools.partial(attn_kernel, win, tile, scale, heads_here),
        out_shape=jax.ShapeDtypeStruct((tok_dev, pw), jnp.bfloat16),
        grid_spec=pltpu.PrefetchScalarGridSpec(
            num_scalar_prefetch=3,
            grid=(tile_dev,),
            in_specs=in_specs,
            out_specs=pl.BlockSpec(blk, q_map),
        ),
        cost_estimate=cost,
    )(win_flat, vcw_flat, vc_own, q_tile, *([kv_ext] * (2 * win)))


def pack_kernel(head_count, chunk_width, col0, table_ref, *refs):
    o_ref = refs[-1]
    for h in range(head_count):
        for t in range(3):
            x_ref = refs[t * head_count + h]
            o_ref[h, :, t * chunk_width : (t + 1) * chunk_width] = x_ref[:, col0 : col0 + chunk_width]


def pack(xs, table, col0, seq_count, head_count, share, chunk_width):
    rows_here, width = xs[0].shape
    part_width = width // head_count

    def in_map(h, d, table_ref):
        return (table_ref[d * head_count + h], h)

    in_specs = [
        pl.BlockSpec((share, part_width), functools.partial(in_map, h))
        for t in range(3)
        for h in range(head_count)
    ]
    return pl.pallas_call(
        functools.partial(pack_kernel, head_count, chunk_width, col0),
        out_shape=jax.ShapeDtypeStruct((seq_count * head_count, share, 3 * chunk_width), xs[0].dtype),
        grid_spec=pltpu.PrefetchScalarGridSpec(
            num_scalar_prefetch=1,
            grid=(seq_count,),
            in_specs=in_specs,
            out_specs=pl.BlockSpec((head_count, share, 3 * chunk_width), lambda d, table_ref: (d, 0, 0)),
        ),
        cost_estimate=pl.CostEstimate(
            flops=0, transcendentals=0, bytes_accessed=2 * 3 * rows_here * head_count * chunk_width * 2
        ),
    )(table, *[x for x in xs for h in range(head_count)])


def unpack_kernel(head_count, part_width, chunk_widths, table_ref, *refs):
    o_ref = refs[-1]
    col0 = 0
    for c, chunk_width in enumerate(chunk_widths):
        for h in range(head_count):
            base = h * part_width + col0
            o_ref[:, base : base + chunk_width] = refs[c * head_count + h][0]
        col0 += chunk_width


def unpack(backs, table, seq_count, head_count, share, width):
    part_width = width // head_count

    def in_map(h, o, table_ref):
        return (table_ref[o * head_count + h], 0, 0)

    in_specs = [
        pl.BlockSpec((1, share, b.shape[2]), functools.partial(in_map, h))
        for b in backs
        for h in range(head_count)
    ]
    return pl.pallas_call(
        functools.partial(unpack_kernel, head_count, part_width, tuple(b.shape[2] for b in backs)),
        out_shape=jax.ShapeDtypeStruct((seq_count * share, width), backs[0].dtype),
        grid_spec=pltpu.PrefetchScalarGridSpec(
            num_scalar_prefetch=1,
            grid=(seq_count,),
            in_specs=in_specs,
            out_specs=pl.BlockSpec((share, width), lambda o, table_ref: (o, 0)),
        ),
        cost_estimate=pl.CostEstimate(
            flops=0, transcendentals=0, bytes_accessed=2 * seq_count * share * width * 2
        ),
    )(table, *[b for b in backs for h in range(head_count)])


def body(placements, query, key, value, raster_to_tile, window_list, valid_count):
    seq_count = lax.axis_size("seq")
    head_count = lax.axis_size("head")
    seq_pos = lax.axis_index("seq")
    head_pos = lax.axis_index("head")
    rows_here, width = query.shape
    part_width = width // head_count
    tile_dev, win = window_list.shape
    tok_dev = rows_here * head_count
    tile = tok_dev // tile_dev
    share = rows_here // seq_count
    reach = win - 1
    rim = reach * tile
    ext_tiles = tile_dev + 2 * reach
    heads_here = part_width // HEAD_DIM
    all_tiles = valid_count.shape[0]
    chunks = 2 if heads_here % 2 == 0 else 1
    chunk_heads = heads_here // chunks
    chunk_width = chunk_heads * HEAD_DIM
    devices = seq_count * head_count

    owner_at = [[0] * seq_count for _ in range(head_count)]
    for h in range(head_count):
        for o, d in enumerate(placements[h % len(placements)]):
            owner_at[h][d] = o
    pos_of = [placements[h % len(placements)] for h in range(head_count)]
    send_blocks = [owner_at[h][d] * head_count + h for d in range(seq_count) for h in range(head_count)]
    back_blocks = [pos_of[h][o] * head_count + h for o in range(seq_count) for h in range(head_count)]
    owner_rows = jnp.array(
        [owner_at[h][d] for d in range(seq_count) for h in range(head_count)], jnp.int32
    )
    send_blocks = jnp.array(send_blocks, jnp.int32)
    back_blocks = jnp.array(back_blocks, jnp.int32)
    send_order = jnp.argsort(raster_to_tile)
    slots_sorted = raster_to_tile[send_order].reshape(seq_count, share)
    slot_send = jnp.broadcast_to(slots_sorted[:, None, :], (seq_count, head_count, share))
    slot_send = slot_send.reshape(devices, share)[send_blocks]
    slot_in = lax.all_to_all(
        slot_send, ("seq", "head"), split_axis=0, concat_axis=0, tiled=True
    ).reshape(tok_dev)
    my_owner = jnp.array(owner_at, jnp.int32)[head_pos, seq_pos]
    local = slot_in - my_owner * tok_dev
    place = jnp.zeros((tok_dev,), jnp.int32).at[local].set(jnp.arange(tok_dev, dtype=jnp.int32))
    route = (local[:, None] == jnp.arange(tok_dev, dtype=jnp.int32)[None, :]).astype(query.dtype)

    both = ("seq", "head")
    window_mine = lax.ppermute(
        window_list,
        both,
        [(o * head_count + h, pos_of[h][o] * head_count + h) for o in range(seq_count) for h in range(head_count)],
    )
    first_tile = my_owner * tile_dev - reach
    global_tiles = jnp.clip(first_tile + jnp.arange(ext_tiles, dtype=jnp.int32), 0, all_tiles - 1)
    vc_ext = valid_count[global_tiles]
    local_windows = (window_mine - first_tile).astype(jnp.int32)
    win_flat = local_windows.reshape(tile_dev * win)
    vcw_flat = vc_ext[local_windows].reshape(tile_dev * win)
    vc_own = vc_ext[reach : reach + tile_dev]

    to_right = [
        (pos_of[h][o] * head_count + h, pos_of[h][o + 1] * head_count + h)
        for o in range(seq_count - 1)
        for h in range(head_count)
    ]
    to_left = [(b, a) for a, b in to_right]

    packable = share % 16 == 0
    if packable:
        pick = (send_order[:, None] == jnp.arange(rows_here, dtype=jnp.int32)[None, :]).astype(query.dtype)
        rows_flat = [jnp.dot(pick, x) for x in (query, key, value)]
    else:
        rows_sorted = [
            x[send_order].reshape(seq_count, share, head_count, chunks, chunk_width)
            for x in (query, key, value)
        ]
    arrived = []
    for c in range(chunks):
        if packable:
            send = pack(rows_flat, owner_rows, c * chunk_width, seq_count, head_count, share, chunk_width)
        else:
            send = jnp.concatenate([x[:, :, :, c, :] for x in rows_sorted], axis=3)
            send = jnp.swapaxes(send, 1, 2).reshape(devices, share, 3 * chunk_width)[send_blocks]
        got = lax.all_to_all(send, both, split_axis=0, concat_axis=0, tiled=True)
        if packable:
            got_tile = lax.dot_general(
                route, got.reshape(tok_dev, 3 * chunk_width), (((0,), (0,)), ((), ()))
            )
        else:
            got_tile = got.reshape(tok_dev, 3 * chunk_width)[place]
        q_tile = got_tile[:, :chunk_width]
        kv_tile = got_tile[:, chunk_width:]
        from_left = lax.ppermute(kv_tile[tok_dev - rim :], both, to_right)
        from_right = lax.ppermute(kv_tile[:rim], both, to_left)
        kv_ext = jnp.concatenate([from_left, kv_tile, from_right], axis=0)
        out_tile = attention(q_tile, kv_ext, win_flat, vcw_flat, vc_own, tile, win, chunk_heads)
        if packable:
            outgoing = jnp.dot(route, out_tile).reshape(devices, share, chunk_width)
        else:
            outgoing = out_tile[local].reshape(devices, share, chunk_width)
        back = lax.all_to_all(outgoing, ("seq", "head"), split_axis=0, concat_axis=0, tiled=True)
        arrived.append(back)
    if packable:
        sorted_rows = unpack(arrived, back_blocks, seq_count, head_count, share, width)
    else:
        arrived = [b[back_blocks] for b in arrived]
        arrived = [b.reshape(seq_count, head_count, share, 1, chunk_width) for b in arrived]
        arrived = jnp.concatenate(arrived, axis=3)
        sorted_rows = jnp.swapaxes(arrived, 1, 2).reshape(rows_here, width)
    inverse = (
        jnp.zeros((rows_here,), jnp.int32).at[send_order].set(jnp.arange(rows_here, dtype=jnp.int32))
    )
    if packable:
        return lax.dot_general(pick, sorted_rows, (((0,), (0,)), ((), ())))
    return sorted_rows[inverse]


def snake(mesh, mirror):
    seq_count = mesh.shape["seq"]
    first = mesh.devices.reshape(seq_count, -1)[:, 0]
    try:
        spots = [tuple(d.coords) for d in first]
    except AttributeError:
        spots = [(0, d % 2, d // 2) for d in range(seq_count)]
    low_z = min(c[2] for c in spots)
    high_y = max(c[1] for c in spots)

    def rank(d):
        x, y, z = spots[d][:3]
        if mirror:
            y = high_y - y
        return (z, y if (z - low_z) % 2 == 0 else -y, x)

    return tuple(sorted(range(seq_count), key=rank))


def solution(mesh):
    placed = (
        P(("seq", "head"), None),
        P(("seq", "head"), None),
        P(("seq", "head"), None),
        P(("seq", "head")),
        P("seq", None),
        P(),
    )
    return jax.shard_map(
        functools.partial(body, (snake(mesh, False), snake(mesh, True))), mesh=mesh, in_specs=placed, out_specs=P(("seq", "head"), None), check_vma=False
    )
```

```python
import functools

import jax
import jax.numpy as jnp
from jax import lax
from jax.experimental import pallas as pl
from jax.experimental.pallas import tpu as pltpu
from jax.sharding import PartitionSpec as P

HEAD_DIM = 128


def attn_kernel(win, tile, scale, heads, win_ref, vcw_ref, vco_ref, q_ref, *refs):
    k_refs = refs[:win]
    v_refs = refs[win : 2 * win]
    o_ref = refs[2 * win]
    i = pl.program_id(0)
    col = lax.broadcasted_iota(jnp.int32, (1, tile), 1)
    row = lax.broadcasted_iota(jnp.int32, (tile, 1), 0)
    for hh in range(heads):
        cols = slice(hh * HEAD_DIM, (hh + 1) * HEAD_DIM)
        q = q_ref[:, cols]
        scores = []
        top = None
        for w in range(win):
            s = lax.dot_general(
                q, k_refs[w][:, cols], (((1,), (1,)), ((), ())), preferred_element_type=jnp.float32
            )
            s = s * scale
            s = jnp.where(col < vcw_ref[i * win + w], s, -jnp.inf)
            scores.append(s)
            m = jnp.max(s, axis=1, keepdims=True)
            top = m if top is None else jnp.maximum(top, m)
        total = None
        acc = None
        for w in range(win):
            p = jnp.exp(scores[w] - top)
            part = jnp.sum(p, axis=1, keepdims=True)
            mix = jnp.dot(
                p.astype(jnp.bfloat16), v_refs[w][:, cols], preferred_element_type=jnp.float32
            )
            total = part if total is None else total + part
            acc = mix if acc is None else acc + mix
        out = acc / total
        out = jnp.where(row < vco_ref[i], out, 0.0)
        o_ref[:, cols] = out.astype(o_ref.dtype)


def attention(q_tile, kv_ext, win_flat, vcw_flat, vc_own, tile, win, heads_here):
    tok_dev, pw = q_tile.shape
    tile_dev = tok_dev // tile
    scale = HEAD_DIM ** (-0.5)

    def q_map(i, w_ref, a_ref, b_ref):
        return (i, 0)

    def k_map(w, i, w_ref, a_ref, b_ref):
        return (w_ref[i * win + w], 0)

    def v_map(w, i, w_ref, a_ref, b_ref):
        return (w_ref[i * win + w], 1)

    blk = (tile, pw)
    in_specs = [pl.BlockSpec(blk, q_map)]
    in_specs += [pl.BlockSpec(blk, functools.partial(k_map, w)) for w in range(win)]
    in_specs += [pl.BlockSpec(blk, functools.partial(v_map, w)) for w in range(win)]
    steps = tile_dev * heads_here
    cost = pl.CostEstimate(
        flops=steps * 4 * tile * win * tile * HEAD_DIM,
        transcendentals=steps * tile * win * tile,
        bytes_accessed=steps * (2 * win + 2) * tile * HEAD_DIM * 2,
    )
    return pl.pallas_call(
        functools.partial(attn_kernel, win, tile, scale, heads_here),
        out_shape=jax.ShapeDtypeStruct((tok_dev, pw), jnp.bfloat16),
        grid_spec=pltpu.PrefetchScalarGridSpec(
            num_scalar_prefetch=3,
            grid=(tile_dev,),
            in_specs=in_specs,
            out_specs=pl.BlockSpec(blk, q_map),
        ),
        cost_estimate=cost,
    )(win_flat, vcw_flat, vc_own, q_tile, *([kv_ext] * (2 * win)))


def pack_kernel(head_count, chunk_width, col0, table_ref, *refs):
    o_ref = refs[-1]
    for h in range(head_count):
        for t in range(3):
            x_ref = refs[t * head_count + h]
            o_ref[h, :, t * chunk_width : (t + 1) * chunk_width] = x_ref[:, col0 : col0 + chunk_width]


def pack(xs, table, col0, seq_count, head_count, share, chunk_width):
    rows_here, width = xs[0].shape
    part_width = width // head_count

    def in_map(h, d, table_ref):
        return (table_ref[d * head_count + h], h)

    in_specs = [
        pl.BlockSpec((share, part_width), functools.partial(in_map, h))
        for t in range(3)
        for h in range(head_count)
    ]
    return pl.pallas_call(
        functools.partial(pack_kernel, head_count, chunk_width, col0),
        out_shape=jax.ShapeDtypeStruct((seq_count * head_count, share, 3 * chunk_width), xs[0].dtype),
        grid_spec=pltpu.PrefetchScalarGridSpec(
            num_scalar_prefetch=1,
            grid=(seq_count,),
            in_specs=in_specs,
            out_specs=pl.BlockSpec((head_count, share, 3 * chunk_width), lambda d, table_ref: (d, 0, 0)),
        ),
        cost_estimate=pl.CostEstimate(
            flops=0, transcendentals=0, bytes_accessed=2 * 3 * rows_here * head_count * chunk_width * 2
        ),
    )(table, *[x for x in xs for h in range(head_count)])


def unpack_kernel(head_count, part_width, chunk_widths, table_ref, *refs):
    o_ref = refs[-1]
    col0 = 0
    for c, chunk_width in enumerate(chunk_widths):
        for h in range(head_count):
            base = h * part_width + col0
            o_ref[:, base : base + chunk_width] = refs[c * head_count + h][0]
        col0 += chunk_width


def unpack(backs, table, seq_count, head_count, share, width):
    part_width = width // head_count

    def in_map(h, o, table_ref):
        return (table_ref[o * head_count + h], 0, 0)

    in_specs = [
        pl.BlockSpec((1, share, b.shape[2]), functools.partial(in_map, h))
        for b in backs
        for h in range(head_count)
    ]
    return pl.pallas_call(
        functools.partial(unpack_kernel, head_count, part_width, tuple(b.shape[2] for b in backs)),
        out_shape=jax.ShapeDtypeStruct((seq_count * share, width), backs[0].dtype),
        grid_spec=pltpu.PrefetchScalarGridSpec(
            num_scalar_prefetch=1,
            grid=(seq_count,),
            in_specs=in_specs,
            out_specs=pl.BlockSpec((share, width), lambda o, table_ref: (o, 0)),
        ),
        cost_estimate=pl.CostEstimate(
            flops=0, transcendentals=0, bytes_accessed=2 * seq_count * share * width * 2
        ),
    )(table, *[b for b in backs for h in range(head_count)])


def body(placements, query, key, value, raster_to_tile, window_list, valid_count):
    seq_count = lax.axis_size("seq")
    head_count = lax.axis_size("head")
    seq_pos = lax.axis_index("seq")
    head_pos = lax.axis_index("head")
    rows_here, width = query.shape
    part_width = width // head_count
    tile_dev, win = window_list.shape
    tok_dev = rows_here * head_count
    tile = tok_dev // tile_dev
    share = rows_here // seq_count
    reach = win - 1
    rim = reach * tile
    ext_tiles = tile_dev + 2 * reach
    heads_here = part_width // HEAD_DIM
    all_tiles = valid_count.shape[0]
    chunks = 2 if heads_here % 2 == 0 else 1
    chunk_heads = heads_here // chunks
    chunk_width = chunk_heads * HEAD_DIM
    devices = seq_count * head_count

    owner_at = [[0] * seq_count for _ in range(head_count)]
    for h in range(head_count):
        for o, d in enumerate(placements[h % len(placements)]):
            owner_at[h][d] = o
    pos_of = [placements[h % len(placements)] for h in range(head_count)]
    send_blocks = [owner_at[h][d] * head_count + h for d in range(seq_count) for h in range(head_count)]
    back_blocks = [pos_of[h][o] * head_count + h for o in range(seq_count) for h in range(head_count)]
    owner_rows = jnp.array(
        [owner_at[h][d] for d in range(seq_count) for h in range(head_count)], jnp.int32
    )
    send_blocks = jnp.array(send_blocks, jnp.int32)
    back_blocks = jnp.array(back_blocks, jnp.int32)
    send_order = jnp.argsort(raster_to_tile)
    rank = jnp.sum((raster_to_tile[None, :] < raster_to_tile[:, None]).astype(jnp.int32), axis=1)
    chosen = rank[None, :] == jnp.arange(rows_here, dtype=jnp.int32)[:, None]
    slots_sorted = jnp.sum(jnp.where(chosen, raster_to_tile[None, :], 0), axis=1).reshape(seq_count, share)
    slot_send = jnp.broadcast_to(slots_sorted[:, None, :], (seq_count, head_count, share))
    slot_send = slot_send.reshape(devices, share)[send_blocks]
    slot_in = lax.all_to_all(
        slot_send, ("seq", "head"), split_axis=0, concat_axis=0, tiled=True
    ).reshape(tok_dev)
    my_owner = jnp.array(owner_at, jnp.int32)[head_pos, seq_pos]
    local = slot_in - my_owner * tok_dev
    place = jnp.zeros((tok_dev,), jnp.int32).at[local].set(jnp.arange(tok_dev, dtype=jnp.int32))
    route = (local[:, None] == jnp.arange(tok_dev, dtype=jnp.int32)[None, :]).astype(query.dtype)

    both = ("seq", "head")
    window_mine = lax.ppermute(
        window_list,
        both,
        [(o * head_count + h, pos_of[h][o] * head_count + h) for o in range(seq_count) for h in range(head_count)],
    )
    first_tile = my_owner * tile_dev - reach
    global_tiles = jnp.clip(first_tile + jnp.arange(ext_tiles, dtype=jnp.int32), 0, all_tiles - 1)
    vc_ext = valid_count[global_tiles]
    local_windows = (window_mine - first_tile).astype(jnp.int32)
    win_flat = local_windows.reshape(tile_dev * win)
    vcw_flat = vc_ext[local_windows].reshape(tile_dev * win)
    vc_own = vc_ext[reach : reach + tile_dev]

    to_right = [
        (pos_of[h][o] * head_count + h, pos_of[h][o + 1] * head_count + h)
        for o in range(seq_count - 1)
        for h in range(head_count)
    ]
    to_left = [(b, a) for a, b in to_right]

    packable = share % 16 == 0
    if packable:
        pick = chosen.astype(query.dtype)
        rows_flat = [jnp.dot(pick, x) for x in (query, key, value)]
    else:
        rows_sorted = [
            x[send_order].reshape(seq_count, share, head_count, chunks, chunk_width)
            for x in (query, key, value)
        ]
    arrived = []
    for c in range(chunks):
        if packable:
            send = pack(rows_flat, owner_rows, c * chunk_width, seq_count, head_count, share, chunk_width)
        else:
            send = jnp.concatenate([x[:, :, :, c, :] for x in rows_sorted], axis=3)
            send = jnp.swapaxes(send, 1, 2).reshape(devices, share, 3 * chunk_width)[send_blocks]
        got = lax.all_to_all(send, both, split_axis=0, concat_axis=0, tiled=True)
        if packable:
            got_tile = lax.dot_general(
                route, got.reshape(tok_dev, 3 * chunk_width), (((0,), (0,)), ((), ()))
            )
        else:
            got_tile = got.reshape(tok_dev, 3 * chunk_width)[place]
        q_tile = got_tile[:, :chunk_width]
        kv_tile = got_tile[:, chunk_width:]
        from_left = lax.ppermute(kv_tile[tok_dev - rim :], both, to_right)
        from_right = lax.ppermute(kv_tile[:rim], both, to_left)
        kv_ext = jnp.concatenate([from_left, kv_tile, from_right], axis=0)
        out_tile = attention(q_tile, kv_ext, win_flat, vcw_flat, vc_own, tile, win, chunk_heads)
        if packable:
            outgoing = jnp.dot(route, out_tile).reshape(devices, share, chunk_width)
        else:
            outgoing = out_tile[local].reshape(devices, share, chunk_width)
        back = lax.all_to_all(outgoing, ("seq", "head"), split_axis=0, concat_axis=0, tiled=True)
        arrived.append(back)
    if packable:
        sorted_rows = unpack(arrived, back_blocks, seq_count, head_count, share, width)
    else:
        arrived = [b[back_blocks] for b in arrived]
        arrived = [b.reshape(seq_count, head_count, share, 1, chunk_width) for b in arrived]
        arrived = jnp.concatenate(arrived, axis=3)
        sorted_rows = jnp.swapaxes(arrived, 1, 2).reshape(rows_here, width)
    inverse = (
        jnp.zeros((rows_here,), jnp.int32).at[send_order].set(jnp.arange(rows_here, dtype=jnp.int32))
    )
    if packable:
        return lax.dot_general(pick, sorted_rows, (((0,), (0,)), ((), ())))
    return sorted_rows[inverse]


def snake(mesh, mirror):
    seq_count = mesh.shape["seq"]
    first = mesh.devices.reshape(seq_count, -1)[:, 0]
    try:
        spots = [tuple(d.coords) for d in first]
    except AttributeError:
        spots = [(0, d % 2, d // 2) for d in range(seq_count)]
    low_z = min(c[2] for c in spots)
    high_y = max(c[1] for c in spots)

    def rank(d):
        x, y, z = spots[d][:3]
        if mirror:
            y = high_y - y
        return (z, y if (z - low_z) % 2 == 0 else -y, x)

    return tuple(sorted(range(seq_count), key=rank))


def solution(mesh):
    placed = (
        P(("seq", "head"), None),
        P(("seq", "head"), None),
        P(("seq", "head"), None),
        P(("seq", "head")),
        P("seq", None),
        P(),
    )
    return jax.shard_map(
        functools.partial(body, (snake(mesh, False), snake(mesh, True))), mesh=mesh, in_specs=placed, out_specs=P(("seq", "head"), None), check_vma=False
    )
```

```python
import functools

import jax
import jax.numpy as jnp
from jax import lax
from jax.experimental import pallas as pl
from jax.experimental.pallas import tpu as pltpu
from jax.sharding import PartitionSpec as P

HEAD_DIM = 128


def attn_kernel(win, tile, scale, heads, win_ref, vcw_ref, vco_ref, q_ref, *refs):
    k_refs = refs[:win]
    v_refs = refs[win : 2 * win]
    o_ref = refs[2 * win]
    i = pl.program_id(0)
    col = lax.broadcasted_iota(jnp.int32, (1, tile), 1)
    row = lax.broadcasted_iota(jnp.int32, (tile, 1), 0)
    for hh in range(heads):
        cols = slice(hh * HEAD_DIM, (hh + 1) * HEAD_DIM)
        q = q_ref[:, cols]
        scores = []
        top = None
        for w in range(win):
            s = lax.dot_general(
                q, k_refs[w][:, cols], (((1,), (1,)), ((), ())), preferred_element_type=jnp.float32
            )
            s = s * scale
            s = jnp.where(col < vcw_ref[i * win + w], s, -jnp.inf)
            scores.append(s)
            m = jnp.max(s, axis=1, keepdims=True)
            top = m if top is None else jnp.maximum(top, m)
        total = None
        acc = None
        for w in range(win):
            p = jnp.exp(scores[w] - top)
            part = jnp.sum(p, axis=1, keepdims=True)
            mix = jnp.dot(
                p.astype(jnp.bfloat16), v_refs[w][:, cols], preferred_element_type=jnp.float32
            )
            total = part if total is None else total + part
            acc = mix if acc is None else acc + mix
        out = acc / total
        out = jnp.where(row < vco_ref[i], out, 0.0)
        o_ref[:, cols] = out.astype(o_ref.dtype)


def attention(q_tile, kv_ext, win_flat, vcw_flat, vc_own, tile, win, heads_here):
    tok_dev, pw = q_tile.shape
    tile_dev = tok_dev // tile
    scale = HEAD_DIM ** (-0.5)

    def q_map(i, w_ref, a_ref, b_ref):
        return (i, 0)

    def k_map(w, i, w_ref, a_ref, b_ref):
        return (w_ref[i * win + w], 0)

    def v_map(w, i, w_ref, a_ref, b_ref):
        return (w_ref[i * win + w], 1)

    blk = (tile, pw)
    in_specs = [pl.BlockSpec(blk, q_map)]
    in_specs += [pl.BlockSpec(blk, functools.partial(k_map, w)) for w in range(win)]
    in_specs += [pl.BlockSpec(blk, functools.partial(v_map, w)) for w in range(win)]
    steps = tile_dev * heads_here
    cost = pl.CostEstimate(
        flops=steps * 4 * tile * win * tile * HEAD_DIM,
        transcendentals=steps * tile * win * tile,
        bytes_accessed=steps * (2 * win + 2) * tile * HEAD_DIM * 2,
    )
    return pl.pallas_call(
        functools.partial(attn_kernel, win, tile, scale, heads_here),
        out_shape=jax.ShapeDtypeStruct((tok_dev, pw), jnp.bfloat16),
        grid_spec=pltpu.PrefetchScalarGridSpec(
            num_scalar_prefetch=3,
            grid=(tile_dev,),
            in_specs=in_specs,
            out_specs=pl.BlockSpec(blk, q_map),
        ),
        cost_estimate=cost,
        compiler_params=pltpu.CompilerParams(allow_input_fusion=[False] * 4 + [True] * (2 * win)),
    )(win_flat, vcw_flat, vc_own, q_tile, *([kv_ext] * (2 * win)))


def pack_kernel(head_count, chunk_width, col0, table_ref, *refs):
    o_ref = refs[-1]
    for h in range(head_count):
        for t in range(3):
            x_ref = refs[t * head_count + h]
            o_ref[h, :, t * chunk_width : (t + 1) * chunk_width] = x_ref[:, col0 : col0 + chunk_width]


def pack(xs, table, col0, seq_count, head_count, share, chunk_width):
    rows_here, width = xs[0].shape
    part_width = width // head_count

    def in_map(h, d, table_ref):
        return (table_ref[d * head_count + h], h)

    in_specs = [
        pl.BlockSpec((share, part_width), functools.partial(in_map, h))
        for t in range(3)
        for h in range(head_count)
    ]
    return pl.pallas_call(
        functools.partial(pack_kernel, head_count, chunk_width, col0),
        out_shape=jax.ShapeDtypeStruct((seq_count * head_count, share, 3 * chunk_width), xs[0].dtype),
        grid_spec=pltpu.PrefetchScalarGridSpec(
            num_scalar_prefetch=1,
            grid=(seq_count,),
            in_specs=in_specs,
            out_specs=pl.BlockSpec((head_count, share, 3 * chunk_width), lambda d, table_ref: (d, 0, 0)),
        ),
        cost_estimate=pl.CostEstimate(
            flops=0, transcendentals=0, bytes_accessed=2 * 3 * rows_here * head_count * chunk_width * 2
        ),
    )(table, *[x for x in xs for h in range(head_count)])


def unpack_kernel(head_count, part_width, chunk_widths, table_ref, *refs):
    o_ref = refs[-1]
    col0 = 0
    for c, chunk_width in enumerate(chunk_widths):
        for h in range(head_count):
            base = h * part_width + col0
            o_ref[:, base : base + chunk_width] = refs[c * head_count + h][0]
        col0 += chunk_width


def unpack(backs, table, seq_count, head_count, share, width):
    part_width = width // head_count

    def in_map(h, o, table_ref):
        return (table_ref[o * head_count + h], 0, 0)

    in_specs = [
        pl.BlockSpec((1, share, b.shape[2]), functools.partial(in_map, h))
        for b in backs
        for h in range(head_count)
    ]
    return pl.pallas_call(
        functools.partial(unpack_kernel, head_count, part_width, tuple(b.shape[2] for b in backs)),
        out_shape=jax.ShapeDtypeStruct((seq_count * share, width), backs[0].dtype),
        grid_spec=pltpu.PrefetchScalarGridSpec(
            num_scalar_prefetch=1,
            grid=(seq_count,),
            in_specs=in_specs,
            out_specs=pl.BlockSpec((share, width), lambda o, table_ref: (o, 0)),
        ),
        cost_estimate=pl.CostEstimate(
            flops=0, transcendentals=0, bytes_accessed=2 * seq_count * share * width * 2
        ),
    )(table, *[b for b in backs for h in range(head_count)])


def body(placements, query, key, value, raster_to_tile, window_list, valid_count):
    seq_count = lax.axis_size("seq")
    head_count = lax.axis_size("head")
    seq_pos = lax.axis_index("seq")
    head_pos = lax.axis_index("head")
    rows_here, width = query.shape
    part_width = width // head_count
    tile_dev, win = window_list.shape
    tok_dev = rows_here * head_count
    tile = tok_dev // tile_dev
    share = rows_here // seq_count
    reach = win - 1
    rim = reach * tile
    ext_tiles = tile_dev + 2 * reach
    heads_here = part_width // HEAD_DIM
    all_tiles = valid_count.shape[0]
    chunks = 2 if heads_here % 2 == 0 else 1
    chunk_heads = heads_here // chunks
    chunk_width = chunk_heads * HEAD_DIM
    devices = seq_count * head_count

    owner_at = [[0] * seq_count for _ in range(head_count)]
    for h in range(head_count):
        for o, d in enumerate(placements[h % len(placements)]):
            owner_at[h][d] = o
    pos_of = [placements[h % len(placements)] for h in range(head_count)]
    send_blocks = [owner_at[h][d] * head_count + h for d in range(seq_count) for h in range(head_count)]
    back_blocks = [pos_of[h][o] * head_count + h for o in range(seq_count) for h in range(head_count)]
    owner_rows = jnp.array(
        [owner_at[h][d] for d in range(seq_count) for h in range(head_count)], jnp.int32
    )
    send_blocks = jnp.array(send_blocks, jnp.int32)
    back_blocks = jnp.array(back_blocks, jnp.int32)
    send_order = jnp.argsort(raster_to_tile)
    rank = jnp.sum((raster_to_tile[None, :] < raster_to_tile[:, None]).astype(jnp.int32), axis=1)
    chosen = rank[None, :] == jnp.arange(rows_here, dtype=jnp.int32)[:, None]
    slots_sorted = jnp.sum(jnp.where(chosen, raster_to_tile[None, :], 0), axis=1).reshape(seq_count, share)
    slot_send = jnp.broadcast_to(slots_sorted[:, None, :], (seq_count, head_count, share))
    slot_send = slot_send.reshape(devices, share)[send_blocks]
    slot_in = lax.all_to_all(
        slot_send, ("seq", "head"), split_axis=0, concat_axis=0, tiled=True
    ).reshape(tok_dev)
    my_owner = jnp.array(owner_at, jnp.int32)[head_pos, seq_pos]
    local = slot_in - my_owner * tok_dev
    place = jnp.zeros((tok_dev,), jnp.int32).at[local].set(jnp.arange(tok_dev, dtype=jnp.int32))
    route = (local[:, None] == jnp.arange(tok_dev, dtype=jnp.int32)[None, :]).astype(query.dtype)

    both = ("seq", "head")
    window_mine = lax.ppermute(
        window_list,
        both,
        [(o * head_count + h, pos_of[h][o] * head_count + h) for o in range(seq_count) for h in range(head_count)],
    )
    first_tile = my_owner * tile_dev - reach
    global_tiles = jnp.clip(first_tile + jnp.arange(ext_tiles, dtype=jnp.int32), 0, all_tiles - 1)
    vc_ext = valid_count[global_tiles]
    local_windows = (window_mine - first_tile).astype(jnp.int32)
    win_flat = local_windows.reshape(tile_dev * win)
    vcw_flat = vc_ext[local_windows].reshape(tile_dev * win)
    vc_own = vc_ext[reach : reach + tile_dev]

    to_right = [
        (pos_of[h][o] * head_count + h, pos_of[h][o + 1] * head_count + h)
        for o in range(seq_count - 1)
        for h in range(head_count)
    ]
    to_left = [(b, a) for a, b in to_right]

    packable = share % 16 == 0
    if packable:
        pick = chosen.astype(query.dtype)
        rows_flat = [jnp.dot(pick, x) for x in (query, key, value)]
    else:
        rows_sorted = [
            x[send_order].reshape(seq_count, share, head_count, chunks, chunk_width)
            for x in (query, key, value)
        ]
    arrived = []
    for c in range(chunks):
        if packable:
            send = pack(rows_flat, owner_rows, c * chunk_width, seq_count, head_count, share, chunk_width)
        else:
            send = jnp.concatenate([x[:, :, :, c, :] for x in rows_sorted], axis=3)
            send = jnp.swapaxes(send, 1, 2).reshape(devices, share, 3 * chunk_width)[send_blocks]
        got = lax.all_to_all(send, both, split_axis=0, concat_axis=0, tiled=True)
        if packable:
            got_tile = lax.dot_general(
                route, got.reshape(tok_dev, 3 * chunk_width), (((0,), (0,)), ((), ()))
            )
        else:
            got_tile = got.reshape(tok_dev, 3 * chunk_width)[place]
        q_tile = got_tile[:, :chunk_width]
        kv_tile = got_tile[:, chunk_width:]
        from_left = lax.ppermute(kv_tile[tok_dev - rim :], both, to_right)
        from_right = lax.ppermute(kv_tile[:rim], both, to_left)
        kv_ext = jnp.concatenate([from_left, kv_tile, from_right], axis=0)
        out_tile = attention(q_tile, kv_ext, win_flat, vcw_flat, vc_own, tile, win, chunk_heads)
        if packable:
            outgoing = jnp.dot(route, out_tile).reshape(devices, share, chunk_width)
        else:
            outgoing = out_tile[local].reshape(devices, share, chunk_width)
        back = lax.all_to_all(outgoing, ("seq", "head"), split_axis=0, concat_axis=0, tiled=True)
        arrived.append(back)
    if packable:
        sorted_rows = unpack(arrived, back_blocks, seq_count, head_count, share, width)
    else:
        arrived = [b[back_blocks] for b in arrived]
        arrived = [b.reshape(seq_count, head_count, share, 1, chunk_width) for b in arrived]
        arrived = jnp.concatenate(arrived, axis=3)
        sorted_rows = jnp.swapaxes(arrived, 1, 2).reshape(rows_here, width)
    inverse = (
        jnp.zeros((rows_here,), jnp.int32).at[send_order].set(jnp.arange(rows_here, dtype=jnp.int32))
    )
    if packable:
        return lax.dot_general(pick, sorted_rows, (((0,), (0,)), ((), ())))
    return sorted_rows[inverse]


def snake(mesh, mirror):
    seq_count = mesh.shape["seq"]
    first = mesh.devices.reshape(seq_count, -1)[:, 0]
    try:
        spots = [tuple(d.coords) for d in first]
    except AttributeError:
        spots = [(0, d % 2, d // 2) for d in range(seq_count)]
    low_z = min(c[2] for c in spots)
    high_y = max(c[1] for c in spots)

    def rank(d):
        x, y, z = spots[d][:3]
        if mirror:
            y = high_y - y
        return (z, y if (z - low_z) % 2 == 0 else -y, x)

    return tuple(sorted(range(seq_count), key=rank))


def solution(mesh):
    placed = (
        P(("seq", "head"), None),
        P(("seq", "head"), None),
        P(("seq", "head"), None),
        P(("seq", "head")),
        P("seq", None),
        P(),
    )
    return jax.shard_map(
        functools.partial(body, (snake(mesh, False), snake(mesh, True))), mesh=mesh, in_specs=placed, out_specs=P(("seq", "head"), None), check_vma=False
    )
```
